256 devices in a mesh: seq: 64 (over z_hi, y, x, core), tp: 4 (over z_lo).
Axes of the slice: x: 4, y: 4, z: 8 (z_hi: 2, z_lo: 4; z = z_hi * 4 + z_lo), core: 2. Of those that a mesh axis runs over, the one named last changes fastest.
Arguments:
- residual: bfloat16 [32768, 2048], P('seq', 'tp'), may hold values from -6 to 6
- norm_gain: float32 [2048], replicated, may hold values from 0.3 to 3
- query_weight: bfloat16 [2048, 1024], P(None, 'tp'), as said below
- key_weight: bfloat16 [2048, 1024], P(None, 'tp'), as said below
- value_weight: bfloat16 [2048, 1024], P(None, 'tp'), may hold values from -0.375 to 0.375
- out_weight: bfloat16 [1024, 2048], P('tp'), may hold values from -0.1875 to 0.1875
- segment_start: int32 [32768], P('seq'), may hold values from 0 to 32640, as said below
- token_valid: int32 [32768], P('seq'), may hold values from 0 to 1, as said below
- page_slot: int32 [256], P('seq'), may hold values from 4 to 511, as said below
Outputs:
- hidden: bfloat16 [32768, 2048], P('seq', 'tp')
- cache: bfloat16 [512, 128, 2048], P('seq', None, 'tp')
The draws below stay inside these ranges and needn't reach their ends.
Inputs may be any that keep to these rules, and one draw needn't show every extreme that they name: `segment_start`: prompts start at multiples of 128 and are contiguous; each holds at most 8192 tokens and one holds exactly 8192. `token_valid`: zeros form a tail of the last page of a prompt; the first token of every prompt is 1. No two pages share a cache page; page_slot // 8 is the device that holds the page's tokens, or the next device when that one holds tokens of the same prompt. `query_weight`: independent entries whose scale falls as the inverse square root of 2048. `key_weight`: independent entries whose scale falls as the inverse square root of 2048.
All inputs are finite; a program needn't handle non-finite values.
Results may differ from the reference program's by a relative error of at most 0.02.
The reference program's roundings to bfloat16 on the way count: a program that leaves them out, or rounds other values in their place, can miss the bound.
Values may be sent and summed in bfloat16 or wider, within the bound.
No kernel may reach another device: no remote copies, remote signals or barrier semaphores. Data moves between devices by JAX's collectives and lax.ppermute only.
A program may use at most 128 MiB of HBM per device.

```python
import math
import jax
import jax.numpy as jnp
from jax import lax

D = 2048
HEADS = 16
HD = 64
PAGE = 128
TOKENS = 32768
TILES = 256
TILES_DEV = 4
SLOT_DEV = 8
SLOTS = 512
LONGEST = 8192


def shuffled(key, device_count):
    scores = jax.random.randint(key, (device_count, TILES_DEV), 0, 1 << 20)
    scores = scores * TILES_DEV + jnp.arange(TILES_DEV, dtype=jnp.int32)[None, :]
    return jnp.argsort(scores, axis=1).astype(jnp.int32)


def layout(key):
    tile_count = TILES
    longest_tiles = LONGEST // PAGE
    group_key = jax.random.fold_in(key, 11)
    bit_key = jax.random.fold_in(key, 12)
    pad_key = jax.random.fold_in(key, 13)
    place_key = jax.random.fold_in(key, 14)
    move_key = jax.random.fold_in(key, 15)
    shift_key = jax.random.fold_in(key, 16)
    keep_key = jax.random.fold_in(key, 17)
    moved_key = jax.random.fold_in(key, 18)
    tile_ids = jnp.arange(tile_count, dtype=jnp.int32)
    shift = jax.random.randint(shift_key, (), 1, longest_tiles)
    relative = tile_ids - shift
    window_of = jnp.floor_divide(relative, longest_tiles)
    inside = relative - window_of * longest_tiles
    windows = (tile_count - shift) // longest_tiles
    chosen = jax.random.randint(place_key, (), 0, windows)
    exponent = jax.random.randint(group_key, (tile_count // 8 + 1,), 0, 7)
    period = jnp.repeat(jnp.left_shift(jnp.int32(1), exponent), 8)[:tile_count]
    random_bits = jax.random.randint(bit_key, (tile_count,), 0, 1 << 20)
    starts = random_bits % period == 0
    on_grid = inside == 0
    outside_flags = starts | on_grid | (tile_ids == tile_count - 1) | (tile_ids == 0)
    starts = jnp.where(window_of == chosen, on_grid, outside_flags)
    start_tile = lax.cummax(jnp.where(starts, tile_ids, 0))
    seg_ends = jnp.concatenate([starts[1:], jnp.ones((1,), dtype=bool)])
    last_tile = lax.cummin(jnp.where(seg_ends, tile_ids, tile_count), reverse=True)
    padding = jax.random.randint(pad_key, (tile_count,), 0, PAGE)
    in_row = jnp.arange(PAGE, dtype=jnp.int32)
    validity = jnp.logical_not(seg_ends[:, None] & (in_row[None, :] >= PAGE - padding[:, None]))
    segment_ids = jnp.repeat(start_tile * PAGE, PAGE)
    owner_dev = tile_ids // TILES_DEV
    within = tile_ids % TILES_DEV
    device_count = tile_count // TILES_DEV
    keep_order = shuffled(keep_key, device_count)
    moved_order = shuffled(moved_key, device_count)
    keep_place = keep_order[owner_dev, within]
    moved_place = moved_order[owner_dev, within]
    can_move = (owner_dev + 1) * TILES_DEV <= last_tile
    move_next = jax.random.randint(move_key, (tile_count,), 0, 2) * can_move.astype(jnp.int32)
    slots = jnp.where(move_next > 0, (owner_dev + 1) * SLOT_DEV + moved_place, owner_dev * SLOT_DEV + TILES_DEV + keep_place)
    return (segment_ids.astype(jnp.int32), validity.reshape(-1).astype(jnp.int32), slots.astype(jnp.int32))


def draw_segment_start(key, part):
    return layout(key)[0]


def draw_token_valid(key, part):
    return layout(key)[1]


def draw_page_slot(key, part):
    return layout(key)[2]


def projection(key):
    base = jnp.clip(jax.random.normal(key, (D, HEADS * HD), jnp.float32), -4.0, 4.0) * D ** (-0.5)
    return base.astype(jnp.bfloat16)


def draw_query_weight(key, part):
    return projection(jax.random.fold_in(key, 21))


def draw_key_weight(key, part):
    return projection(jax.random.fold_in(key, 22))


def block_levels(key, dims, pieces, low, high):
    level, own = 1.0, jax.random.fold_in(key, 6)
    for dim, shards_of in pieces:
        heights = jnp.exp(jax.random.uniform(jax.random.fold_in(own, dim), (shards_of,), jnp.float32, low / len(pieces), high / len(pieces)))
        level = level * jnp.repeat(heights, dims[dim] // shards_of).reshape([-1 if axis == dim else 1 for axis in range(len(dims))])
    return level


def scatter_about(own_key, shape, deviation, most, cuts=(), kind=jnp.bfloat16):
    result = deviation * jax.random.normal(own_key, shape, jnp.float32)
    if cuts:
        result = result * block_levels(own_key, shape, cuts, -0.22, 0.18)
    return jnp.clip(result, -most, most).astype(kind)


def setup_inputs(seed: int = 0) -> dict:
    arg_keys = jax.random.split(jax.random.key(seed), 10)
    residual = scatter_about(arg_keys[0], (TOKENS, D), 0.5, 6.0, ((0, 64), (1, 4)))
    norm_gain = jnp.clip(jnp.exp(jax.random.uniform(arg_keys[1], (D,), jnp.float32, math.log(0.3), math.log(3.0))), 0.3, 3.0)
    query_weight = draw_query_weight(jax.random.fold_in(arg_keys[9], 71), 0)
    key_weight = draw_key_weight(jax.random.fold_in(arg_keys[9], 71), 0)
    value_weight = scatter_about(arg_keys[4], (D, HEADS * HD), (D // 9) ** -0.5, 0.375, ((1, 4),))
    out_weight = scatter_about(arg_keys[5], (HEADS * HD, D), (HEADS * HD) ** -0.5, 0.1875, ((0, 4),))
    segment_start = draw_segment_start(jax.random.fold_in(arg_keys[9], 71), 0)
    token_valid = draw_token_valid(jax.random.fold_in(arg_keys[9], 71), 0)
    page_slot = draw_page_slot(jax.random.fold_in(arg_keys[9], 71), 0)
    return {"residual": residual, "norm_gain": norm_gain, "query_weight": query_weight, "key_weight": key_weight, "value_weight": value_weight, "out_weight": out_weight, "segment_start": segment_start, "token_valid": token_valid, "page_slot": page_slot}


THETA = 130000.0
EPS = 1e-05

def rotate(inputs, positions):
    half_dim = inputs.shape[-1] // 2
    frequency = THETA ** (-2.0 * jnp.arange(half_dim, dtype=jnp.float32) / inputs.shape[-1])
    angles = positions.astype(jnp.float32)[:, None] * frequency[None, :]
    cosine = jnp.cos(angles)[:, None, :]
    sine_part = jnp.sin(angles)[:, None, :]
    front_half = inputs[..., :half_dim]
    back_half = inputs[..., half_dim:]
    return jnp.concatenate([front_half * cosine - back_half * sine_part, back_half * cosine + front_half * sine_part], axis=-1)

def reference(residual, norm_gain, query_weight, key_weight, value_weight, out_weight, segment_start, token_valid, page_slot):
    token_count = residual.shape[0]
    head_count = query_weight.shape[1] // HD
    widened = residual.astype(jnp.float32)
    mean_sq = lax.optimization_barrier(jnp.mean(widened * widened, axis=1, keepdims=True))
    normed = (widened * lax.rsqrt(mean_sq + EPS) * norm_gain[None, :]).astype(jnp.bfloat16)
    places = jnp.arange(token_count, dtype=jnp.int32)
    offsets = places - segment_start
    queries = jnp.dot(normed, query_weight, preferred_element_type=jnp.float32).reshape(token_count, head_count, HD)
    key_raw = jnp.dot(normed, key_weight, preferred_element_type=jnp.float32).reshape(token_count, head_count, HD)
    value_raw = jnp.dot(normed, value_weight, preferred_element_type=jnp.float32).reshape(token_count, head_count, HD)
    query_rot = lax.optimization_barrier(rotate(queries, offsets).astype(jnp.bfloat16))
    key_rot = lax.optimization_barrier(rotate(key_raw, offsets).astype(jnp.bfloat16))
    values = lax.optimization_barrier(value_raw.astype(jnp.bfloat16))
    key_group = jnp.where(token_valid > 0, segment_start, -1)
    query_block = min(512, token_count)
    window = min(LONGEST + query_block, token_count)
    score_scale = HD ** (-0.5)

    def attend(block_index):
        block_start = block_index * query_block
        key_begin = jnp.clip(block_start + query_block - window, 0, token_count - window).astype(jnp.int32)
        query_part = lax.dynamic_slice_in_dim(query_rot, block_start, query_block, 0).astype(jnp.float32)
        key_part = lax.dynamic_slice_in_dim(key_rot, key_begin, window, 0).astype(jnp.float32)
        value_part = lax.dynamic_slice_in_dim(values, key_begin, window, 0).astype(jnp.float32)
        query_seg = lax.dynamic_slice_in_dim(segment_start, block_start, query_block, 0)
        key_seg = lax.dynamic_slice_in_dim(key_group, key_begin, window, 0)
        query_pos = block_start + jnp.arange(query_block, dtype=jnp.int32)
        key_pos = key_begin + jnp.arange(window, dtype=jnp.int32)
        allowed = (key_seg[None, :] == query_seg[:, None]) & (key_pos[None, :] <= query_pos[:, None])
        scores = jnp.einsum('qhd,khd->hqk', query_part, key_part, precision=lax.Precision.HIGHEST) * score_scale
        masked = jnp.where(allowed[None], scores, -1e+30)
        row_max = lax.optimization_barrier(jnp.max(masked, axis=2, keepdims=True))
        weights = jnp.where(allowed[None], jnp.exp(masked - row_max), 0.0)
        denominator = lax.optimization_barrier(jnp.sum(weights, axis=2))
        rounded = lax.optimization_barrier(weights.astype(jnp.bfloat16)).astype(jnp.float32)
        mixed = jnp.einsum('hqk,khd->qhd', rounded, value_part, precision=lax.Precision.HIGHEST)
        mixed = mixed / jnp.transpose(denominator)[:, :, None]
        return mixed.astype(jnp.bfloat16)
    attended = lax.map(attend, jnp.arange(token_count // query_block, dtype=jnp.int32))
    attended = attended.reshape(token_count, head_count * HD)
    projected = jnp.dot(attended, out_weight, preferred_element_type=jnp.float32)
    hidden = (widened + projected).astype(jnp.bfloat16)
    cache_rows = jnp.concatenate([key_rot[:, :, None, :], values[:, :, None, :]], axis=2).reshape(token_count, head_count * 2 * HD)
    cache_rows = jnp.where(token_valid[:, None] > 0, cache_rows, jnp.zeros_like(cache_rows))
    destination = page_slot[places // PAGE] * PAGE + places % PAGE
    cache = jnp.zeros((SLOTS * PAGE, head_count * 2 * HD), jnp.bfloat16).at[destination].set(cache_rows)
    return (hidden, cache.reshape(SLOTS, PAGE, head_count * 2 * HD))
```

```python
import jax
import jax.numpy as jnp
from jax import lax
from jax.sharding import PartitionSpec as P

HD = 64
PAGE = 128
SPAN = 16


THETA = 130000.0
EPS = 1e-05


def passed_along(x, axis, by):
    count = lax.axis_size(axis)
    pairs = [(i, i + by) for i in range(count) if 0 <= i + by < count]
    return lax.ppermute(x, axis, pairs)


def rotate(inputs, positions):
    half_dim = inputs.shape[-1] // 2
    frequency = THETA ** (-2.0 * jnp.arange(half_dim, dtype=jnp.float32) / inputs.shape[-1])
    angles = positions.astype(jnp.float32)[:, None] * frequency[None, :]
    cosine = jnp.cos(angles)[:, None, :]
    sine_part = jnp.sin(angles)[:, None, :]
    front_half = inputs[..., :half_dim]
    back_half = inputs[..., half_dim:]
    return jnp.concatenate(
        [front_half * cosine - back_half * sine_part, back_half * cosine + front_half * sine_part],
        axis=-1,
    )


def body(
    residual,
    norm_gain,
    query_weight,
    key_weight,
    value_weight,
    out_weight,
    segment_start,
    token_valid,
    page_slot,
):
    row_count = residual.shape[0]
    local_heads = query_weight.shape[1] // HD
    gathered = lax.all_gather(residual, "tp", axis=1, tiled=True)
    widened = gathered.astype(jnp.float32)
    mean_sq = jnp.mean(widened * widened, axis=1, keepdims=True)
    normed = (widened * lax.rsqrt(mean_sq + EPS) * norm_gain[None, :]).astype(jnp.bfloat16)
    seq_rank = lax.axis_index("seq")
    first_row = seq_rank * row_count
    places = first_row + jnp.arange(row_count, dtype=jnp.int32)
    offsets = places - segment_start
    queries = jnp.dot(normed, query_weight, preferred_element_type=jnp.float32).reshape(
        row_count, local_heads, HD
    )
    queries = rotate(queries, offsets).astype(jnp.bfloat16)
    key_rot = jnp.dot(normed, key_weight, preferred_element_type=jnp.float32).reshape(
        row_count, local_heads, HD
    )
    key_rot = rotate(key_rot, offsets).astype(jnp.bfloat16)
    values = (
        jnp.dot(normed, value_weight, preferred_element_type=jnp.float32)
        .reshape(row_count, local_heads, HD)
        .astype(jnp.bfloat16)
    )
    packed = jnp.concatenate([key_rot[:, :, None, :], values[:, :, None, :]], axis=2).reshape(
        row_count, local_heads * 2 * HD
    )
    packed = jnp.where(token_valid[:, None] > 0, packed, jnp.zeros_like(packed))
    score_scale = HD ** (-0.5)

    out_cols = lax.all_to_all(out_weight, "tp", 1, 0, tiled=True)
    prev_slot = passed_along(page_slot, "seq", 1)

    def attend_block(running, incoming, allowed):
        row_max, norm_sum, weighted = running
        key_value = incoming.reshape(incoming.shape[0], local_heads, 2, HD)
        scores = (
            jnp.einsum(
                "qhd,khd->hqk", queries, key_value[:, :, 0, :], preferred_element_type=jnp.float32
            )
            * score_scale
        )
        block_max = jnp.max(jnp.where(allowed[None], scores, -1e30), axis=2)
        new_max = jnp.maximum(row_max, block_max)
        weights = jnp.where(allowed[None], jnp.exp(scores - new_max[:, :, None]), 0.0)
        shrink = jnp.exp(row_max - new_max)
        norm_sum = norm_sum * shrink + jnp.sum(weights, axis=2)
        update = jnp.einsum(
            "hqk,khd->qhd",
            weights.astype(jnp.bfloat16),
            key_value[:, :, 1, :],
            preferred_element_type=jnp.float32,
        )
        weighted = weighted * jnp.transpose(shrink)[:, :, None] + update
        return (new_max, norm_sum, weighted)

    local_pos = jnp.arange(row_count, dtype=jnp.int32)
    own_allowed = (
        ((first_row + local_pos)[None, :] >= segment_start[:, None])
        & (local_pos[None, :] <= local_pos[:, None])
        & (token_valid[None, :] > 0)
    )
    initial = (
        jnp.full((local_heads, row_count), -1e30, jnp.float32),
        jnp.zeros((local_heads, row_count), jnp.float32),
        jnp.zeros((row_count, local_heads, HD), jnp.float32),
    )
    carried = attend_block(initial, packed, own_allowed)

    def remote_absorb(running, incoming, step):
        key_places = first_row - step * row_count + local_pos
        allowed = key_places[None, :] >= segment_start[:, None]
        return attend_block(running, incoming, allowed)

    prev_block = passed_along(packed, "seq", 1)
    carried = remote_absorb(carried, prev_block, 1)
    reach_dev = min(SPAN, lax.axis_size("seq") // 2)

    def advance(step_index, carry_in):
        moving, running = carry_in
        moving = passed_along(moving, "seq", 1)
        running = remote_absorb(running, moving, step_index)
        return (moving, running)

    _, carried = lax.fori_loop(2, reach_dev + 1, advance, (prev_block, carried))
    row_max, norm_sum, weighted = carried
    attended = (
        (weighted / jnp.transpose(norm_sum)[:, :, None])
        .astype(jnp.bfloat16)
        .reshape(row_count, local_heads * HD)
    )

    tiles = page_slot.shape[0]
    slot_count = 2 * tiles
    base_slot = seq_rank * slot_count
    has_prev = seq_rank > 0
    cand_slot = jnp.concatenate([page_slot, jnp.where(has_prev, prev_slot, -1)]) - base_slot
    cand_pages = jnp.concatenate(
        [packed.reshape(tiles, PAGE, -1), prev_block.reshape(tiles, PAGE, -1)], axis=0
    )
    match = cand_slot[None, :] == jnp.arange(slot_count, dtype=jnp.int32)[:, None]
    pick = jnp.argmax(match.astype(jnp.int32), axis=1)
    found = jnp.any(match, axis=1)
    cache_pages = jnp.where(found[:, None, None], cand_pages[pick], jnp.zeros_like(cand_pages[:1]))

    attended_all = lax.all_gather(attended, "tp", axis=1, tiled=True)
    projected = jnp.dot(attended_all, out_cols, preferred_element_type=jnp.float32)
    hidden = (residual.astype(jnp.float32) + projected).astype(jnp.bfloat16)
    return (hidden, cache_pages)


def solution(mesh):
    return jax.shard_map(
        body,
        mesh=mesh,
        in_specs=(
            P("seq", "tp"),
            P(),
            P(None, "tp"),
            P(None, "tp"),
            P(None, "tp"),
            P("tp", None),
            P("seq"),
            P("seq"),
            P("seq"),
        ),
        out_specs=(P("seq", "tp"), P("seq", None, "tp")),
        check_vma=False,
    )
```

```python
import jax
import jax.numpy as jnp
from jax import lax
from jax.sharding import PartitionSpec as P

HD = 64
PAGE = 128
SPAN = 16


THETA = 130000.0
EPS = 1e-05


def passed_along(x, axis, by):
    count = lax.axis_size(axis)
    pairs = [(i, i + by) for i in range(count) if 0 <= i + by < count]
    return lax.ppermute(x, axis, pairs)


def rotate(inputs, positions):
    half_dim = inputs.shape[-1] // 2
    frequency = THETA ** (-2.0 * jnp.arange(half_dim, dtype=jnp.float32) / inputs.shape[-1])
    angles = positions.astype(jnp.float32)[:, None] * frequency[None, :]
    cosine = jnp.cos(angles)[:, None, :]
    sine_part = jnp.sin(angles)[:, None, :]
    front_half = inputs[..., :half_dim]
    back_half = inputs[..., half_dim:]
    return jnp.concatenate(
        [front_half * cosine - back_half * sine_part, back_half * cosine + front_half * sine_part],
        axis=-1,
    )


def body(
    residual,
    norm_gain,
    query_weight,
    key_weight,
    value_weight,
    out_weight,
    segment_start,
    token_valid,
    page_slot,
):
    row_count = residual.shape[0]
    local_heads = query_weight.shape[1] // HD
    gathered = lax.all_gather(residual, "tp", axis=1, tiled=True)
    widened = gathered.astype(jnp.float32)
    mean_sq = jnp.mean(widened * widened, axis=1, keepdims=True)
    normed = (widened * lax.rsqrt(mean_sq + EPS) * norm_gain[None, :]).astype(jnp.bfloat16)
    seq_rank = lax.axis_index("seq")
    first_row = seq_rank * row_count
    places = first_row + jnp.arange(row_count, dtype=jnp.int32)
    offsets = places - segment_start
    queries = jnp.dot(normed, query_weight, preferred_element_type=jnp.float32).reshape(
        row_count, local_heads, HD
    )
    queries = rotate(queries, offsets).astype(jnp.bfloat16)
    key_rot = jnp.dot(normed, key_weight, preferred_element_type=jnp.float32).reshape(
        row_count, local_heads, HD
    )
    key_rot = rotate(key_rot, offsets).astype(jnp.bfloat16)
    values = (
        jnp.dot(normed, value_weight, preferred_element_type=jnp.float32)
        .reshape(row_count, local_heads, HD)
        .astype(jnp.bfloat16)
    )
    packed = jnp.concatenate([key_rot[:, :, None, :], values[:, :, None, :]], axis=2).reshape(
        row_count, local_heads * 2 * HD
    )
    packed = jnp.where(token_valid[:, None] > 0, packed, jnp.zeros_like(packed))
    score_scale = HD ** (-0.5)

    out_cols = lax.all_to_all(out_weight, "tp", 1, 0, tiled=True)
    prev_slot = passed_along(page_slot, "seq", 1)

    def attend_block(running, incoming, allowed):
        row_max, norm_sum, weighted = running
        key_value = incoming.reshape(incoming.shape[0], local_heads, 2, HD)
        scores = (
            jnp.einsum(
                "qhd,khd->hqk", queries, key_value[:, :, 0, :], preferred_element_type=jnp.float32
            )
            * score_scale
        )
        block_max = jnp.max(jnp.where(allowed[None], scores, -1e30), axis=2)
        new_max = jnp.maximum(row_max, block_max)
        weights = jnp.where(allowed[None], jnp.exp(scores - new_max[:, :, None]), 0.0)
        shrink = jnp.exp(row_max - new_max)
        norm_sum = norm_sum * shrink + jnp.sum(weights, axis=2)
        update = jnp.einsum(
            "hqk,khd->qhd",
            weights.astype(jnp.bfloat16),
            key_value[:, :, 1, :],
            preferred_element_type=jnp.float32,
        )
        weighted = weighted * jnp.transpose(shrink)[:, :, None] + update
        return (new_max, norm_sum, weighted)

    local_pos = jnp.arange(row_count, dtype=jnp.int32)
    own_valid = token_valid > 0

    def absorb(running, incoming, step):
        key_places = first_row - step * row_count + local_pos
        key_ok = own_valid | (step > 0)
        allowed = (
            (key_places[None, :] >= segment_start[:, None])
            & (key_places[None, :] <= places[:, None])
            & key_ok[None, :]
        )
        return attend_block(running, incoming, allowed)

    initial = (
        jnp.full((local_heads, row_count), -1e30, jnp.float32),
        jnp.zeros((local_heads, row_count), jnp.float32),
        jnp.zeros((row_count, local_heads, HD), jnp.float32),
    )
    seq_count = lax.axis_size("seq")
    reach_dev = min(SPAN, seq_count // 2)
    half = seq_count // 2
    chain = [(i, i + 1) for i in range(seq_count - 1)]
    inner = [p for p in chain if p != (half - 1, half)]
    first_block = segment_start[0] // row_count
    cross_here = jnp.clip(seq_rank - first_block, 0, reach_dev).astype(jnp.int32)
    cross_steps = lax.psum(jnp.where(seq_rank == half, cross_here, 0), "seq")
    cross_steps = jnp.maximum(cross_steps, 1)

    prev_block = lax.ppermute(packed, "seq", chain)
    carried = absorb(initial, packed, 0)

    def step_with(pairs):
        def advance(step_index, carry_in):
            held, running = carry_in
            sent = lax.ppermute(held, "seq", pairs)
            running = absorb(running, held, step_index)
            return (sent, running)

        return advance

    held, carried = lax.fori_loop(1, cross_steps, step_with(chain), (prev_block, carried))
    held, carried = lax.fori_loop(cross_steps, reach_dev, step_with(inner), (held, carried))
    carried = absorb(carried, held, reach_dev)
    row_max, norm_sum, weighted = carried
    attended = (
        (weighted / jnp.transpose(norm_sum)[:, :, None])
        .astype(jnp.bfloat16)
        .reshape(row_count, local_heads * HD)
    )

    tiles = page_slot.shape[0]
    slot_count = 2 * tiles
    base_slot = seq_rank * slot_count
    has_prev = seq_rank > 0
    cand_slot = jnp.concatenate([page_slot, jnp.where(has_prev, prev_slot, -1)]) - base_slot
    cand_pages = jnp.concatenate(
        [packed.reshape(tiles, PAGE, -1), prev_block.reshape(tiles, PAGE, -1)], axis=0
    )
    match = cand_slot[None, :] == jnp.arange(slot_count, dtype=jnp.int32)[:, None]
    pick = jnp.argmax(match.astype(jnp.int32), axis=1)
    found = jnp.any(match, axis=1)
    cache_pages = jnp.where(found[:, None, None], cand_pages[pick], jnp.zeros_like(cand_pages[:1]))

    attended_all = lax.all_gather(attended, "tp", axis=1, tiled=True)
    projected = jnp.dot(attended_all, out_cols, preferred_element_type=jnp.float32)
    hidden = (residual.astype(jnp.float32) + projected).astype(jnp.bfloat16)
    return (hidden, cache_pages)


def solution(mesh):
    return jax.shard_map(
        body,
        mesh=mesh,
        in_specs=(
            P("seq", "tp"),
            P(),
            P(None, "tp"),
            P(None, "tp"),
            P(None, "tp"),
            P("tp", None),
            P("seq"),
            P("seq"),
            P("seq"),
        ),
        out_specs=(P("seq", "tp"), P("seq", None, "tp")),
        check_vma=False,
    )
```

```python
import jax
import jax.numpy as jnp
from jax import lax
from jax.experimental import pallas as pl
from jax.experimental.pallas import tpu as pltpu
from jax.sharding import PartitionSpec as P

HD = 64
PAGE = 128
SPAN = 16


THETA = 130000.0
EPS = 1e-05
SCALE = HD ** (-0.5)


def _step_kernel(kstart_ref, kbias_ref, seg_ref, tpos_ref, q_ref, kv_ref, s_ref, out_ref):
    q = q_ref[...]
    kv = kv_ref[...]
    rows, width = out_ref.shape
    keys = kv.shape[0]
    scores = lax.dot_general(
        q, kv[:, :HD], (((1,), (1,)), ((), ())), preferred_element_type=jnp.float32
    ) * SCALE
    krow = kstart_ref[0] + lax.broadcasted_iota(jnp.int32, (1, keys), 1) + kbias_ref[...]
    allowed = (krow >= seg_ref[...]) & (krow <= tpos_ref[...])
    state = s_ref[...]
    m_old = state[:, 0:1]
    l_old = state[:, 1:2]
    block_max = jnp.max(jnp.where(allowed, scores, -1e30), axis=1, keepdims=True)
    m_new = jnp.maximum(m_old, block_max)
    weights = jnp.where(allowed, jnp.exp(scores - m_new), 0.0)
    shrink = jnp.exp(m_old - m_new)
    l_new = l_old * shrink + jnp.sum(weights, axis=1, keepdims=True)
    update = jnp.dot(weights.astype(jnp.bfloat16), kv, preferred_element_type=jnp.float32)
    lane = lax.broadcasted_iota(jnp.int32, (rows, width), 1)
    acc = state * shrink + update
    out_ref[...] = jnp.where(lane >= HD, acc, jnp.where(lane == 0, m_new, jnp.where(lane == 1, l_new, 0.0)))


def attend_step(kstart, kbias, seg_col, tpos_col, q_hm, kv_hm, state):
    heads, rows, _ = q_hm.shape
    keys = kv_hm.shape[1]
    width = kv_hm.shape[2]
    grid_spec = pltpu.PrefetchScalarGridSpec(
        num_scalar_prefetch=1,
        grid=(heads,),
        in_specs=[
            pl.BlockSpec((1, keys), lambda h, ks: (0, 0)),
            pl.BlockSpec((rows, 1), lambda h, ks: (0, 0)),
            pl.BlockSpec((rows, 1), lambda h, ks: (0, 0)),
            pl.BlockSpec((None, rows, HD), lambda h, ks: (h, 0, 0)),
            pl.BlockSpec((None, keys, width), lambda h, ks: (h, 0, 0)),
            pl.BlockSpec((None, rows, width), lambda h, ks: (h, 0, 0)),
        ],
        out_specs=pl.BlockSpec((None, rows, width), lambda h, ks: (h, 0, 0)),
    )
    flops = heads * rows * keys * (2 * HD + 2 * width)
    return pl.pallas_call(
        _step_kernel,
        grid_spec=grid_spec,
        out_shape=jax.ShapeDtypeStruct(state.shape, jnp.float32),
        input_output_aliases={6: 0},
        cost_estimate=pl.CostEstimate(
            flops=flops,
            transcendentals=heads * rows * keys,
            bytes_accessed=q_hm.size * 2 + kv_hm.size * 2 + state.size * 8,
        ),
    )(kstart, kbias, seg_col, tpos_col, q_hm, kv_hm, state)


def passed_along(x, axis, by):
    count = lax.axis_size(axis)
    pairs = [(i, i + by) for i in range(count) if 0 <= i + by < count]
    return lax.ppermute(x, axis, pairs)


def rotate(inputs, positions):
    half_dim = inputs.shape[-1] // 2
    frequency = THETA ** (-2.0 * jnp.arange(half_dim, dtype=jnp.float32) / inputs.shape[-1])
    angles = positions.astype(jnp.float32)[:, None] * frequency[None, :]
    cosine = jnp.cos(angles)[:, None, :]
    sine_part = jnp.sin(angles)[:, None, :]
    front_half = inputs[..., :half_dim]
    back_half = inputs[..., half_dim:]
    return jnp.concatenate(
        [front_half * cosine - back_half * sine_part, back_half * cosine + front_half * sine_part],
        axis=-1,
    )


def body(
    residual,
    norm_gain,
    query_weight,
    key_weight,
    value_weight,
    out_weight,
    segment_start,
    token_valid,
    page_slot,
):
    row_count = residual.shape[0]
    local_heads = query_weight.shape[1] // HD
    gathered = lax.all_gather(residual, "tp", axis=1, tiled=True)
    widened = gathered.astype(jnp.float32)
    mean_sq = jnp.mean(widened * widened, axis=1, keepdims=True)
    normed = (widened * lax.rsqrt(mean_sq + EPS) * norm_gain[None, :]).astype(jnp.bfloat16)
    seq_rank = lax.axis_index("seq")
    first_row = seq_rank * row_count
    places = first_row + jnp.arange(row_count, dtype=jnp.int32)
    offsets = places - segment_start
    queries = jnp.dot(normed, query_weight, preferred_element_type=jnp.float32).reshape(
        row_count, local_heads, HD
    )
    queries = rotate(queries, offsets).astype(jnp.bfloat16)
    key_rot = jnp.dot(normed, key_weight, preferred_element_type=jnp.float32).reshape(
        row_count, local_heads, HD
    )
    key_rot = rotate(key_rot, offsets).astype(jnp.bfloat16)
    values = (
        jnp.dot(normed, value_weight, preferred_element_type=jnp.float32)
        .reshape(row_count, local_heads, HD)
        .astype(jnp.bfloat16)
    )
    packed = jnp.concatenate([key_rot[:, :, None, :], values[:, :, None, :]], axis=2).reshape(
        row_count, local_heads * 2 * HD
    )
    packed = jnp.where(token_valid[:, None] > 0, packed, jnp.zeros_like(packed))

    out_cols = lax.all_to_all(out_weight, "tp", 1, 0, tiled=True)
    prev_slot = passed_along(page_slot, "seq", 1)

    q_hm = jnp.transpose(queries, (1, 0, 2))
    kv_hm = jnp.transpose(packed.reshape(row_count, local_heads, 2 * HD), (1, 0, 2))
    seg_col = segment_start[:, None]
    tpos_col = places[:, None]
    own_bias = jnp.where(token_valid > 0, 0, 1 << 30).astype(jnp.int32)[None, :]
    remote_bias = jnp.zeros((1, row_count), jnp.int32)

    def absorb(state, incoming, step, bias):
        kstart = (first_row - step * row_count).astype(jnp.int32).reshape(1)
        return attend_step(kstart, bias, seg_col, tpos_col, q_hm, incoming, state)

    lane = jnp.arange(2 * HD, dtype=jnp.int32)
    initial = jnp.broadcast_to(
        jnp.where(lane == 0, -1e30, 0.0).astype(jnp.float32), (local_heads, row_count, 2 * HD)
    )
    seq_count = lax.axis_size("seq")
    reach_dev = min(SPAN, seq_count // 2)
    half = seq_count // 2
    chain = [(i, i + 1) for i in range(seq_count - 1)]
    inner = [p for p in chain if p != (half - 1, half)]
    first_block = segment_start[0] // row_count
    cross_here = jnp.clip(seq_rank - first_block, 0, reach_dev).astype(jnp.int32)
    cross_steps = lax.psum(jnp.where(seq_rank == half, cross_here, 0), "seq")
    cross_steps = jnp.maximum(cross_steps, 1)

    prev_block = lax.ppermute(kv_hm, "seq", chain)
    carried = absorb(initial, kv_hm, 0, own_bias)

    def step_with(pairs):
        def advance(step_index, carry_in):
            held, state = carry_in
            sent = lax.ppermute(held, "seq", pairs)
            state = absorb(state, held, step_index, remote_bias)
            return (sent, state)

        return advance

    held, carried = lax.fori_loop(1, cross_steps, step_with(chain), (prev_block, carried))
    held, carried = lax.fori_loop(cross_steps, reach_dev, step_with(inner), (held, carried))
    carried = absorb(carried, held, reach_dev, remote_bias)
    attended = (
        jnp.transpose(carried[:, :, HD:] / carried[:, :, 1:2], (1, 0, 2))
        .astype(jnp.bfloat16)
        .reshape(row_count, local_heads * HD)
    )

    tiles = page_slot.shape[0]
    slot_count = 2 * tiles
    base_slot = seq_rank * slot_count
    has_prev = seq_rank > 0
    cand_slot = jnp.concatenate([page_slot, jnp.where(has_prev, prev_slot, -1)]) - base_slot
    cand_pages = jnp.concatenate(
        [packed.reshape(tiles, PAGE, -1), jnp.transpose(prev_block, (1, 0, 2)).reshape(tiles, PAGE, -1)],
        axis=0,
    )
    match = cand_slot[None, :] == jnp.arange(slot_count, dtype=jnp.int32)[:, None]
    pick = jnp.argmax(match.astype(jnp.int32), axis=1)
    found = jnp.any(match, axis=1)
    cache_pages = jnp.where(found[:, None, None], cand_pages[pick], jnp.zeros_like(cand_pages[:1]))

    attended_all = lax.all_gather(attended, "tp", axis=1, tiled=True)
    projected = jnp.dot(attended_all, out_cols, preferred_element_type=jnp.float32)
    hidden = (residual.astype(jnp.float32) + projected).astype(jnp.bfloat16)
    return (hidden, cache_pages)


def solution(mesh):
    return jax.shard_map(
        body,
        mesh=mesh,
        in_specs=(
            P("seq", "tp"),
            P(),
            P(None, "tp"),
            P(None, "tp"),
            P(None, "tp"),
            P("tp", None),
            P("seq"),
            P("seq"),
            P("seq"),
        ),
        out_specs=(P("seq", "tp"), P("seq", None, "tp")),
        check_vma=False,
    )
```

```python
import jax
import jax.numpy as jnp
from jax import lax
from jax.experimental import pallas as pl
from jax.experimental.pallas import tpu as pltpu
from jax.sharding import PartitionSpec as P

HD = 64
PAGE = 128
SPAN = 16


THETA = 130000.0
EPS = 1e-05
SCALE = HD ** (-0.5)
FAR = 1 << 30


def _step_kernel(info_ref, valid_ref, seg_ref, q_ref, kv_ref, s_ref, out_ref):
    kstart = info_ref[0]
    qstart = info_ref[1]
    check_valid = info_ref[2]
    seg_last = info_ref[3]
    rows, width = out_ref.shape
    keys = kv_ref.shape[0]
    seg_first = seg_ref[0, 0]
    none_allowed = kstart + keys - 1 < seg_first
    all_allowed = (seg_last <= kstart) & (kstart + keys - 1 <= qstart) & (check_valid == 0)

    def update(allowed):
        q = q_ref[...]
        kv = kv_ref[...]
        scores = lax.dot_general(
            q, kv[:, :HD], (((1,), (1,)), ((), ())), preferred_element_type=jnp.float32
        ) * SCALE
        state = s_ref[...]
        m_old = state[:, 0:1]
        l_old = state[:, 1:2]
        if allowed is None:
            block_max = jnp.max(scores, axis=1, keepdims=True)
        else:
            block_max = jnp.max(jnp.where(allowed, scores, -1e30), axis=1, keepdims=True)
        m_new = jnp.maximum(m_old, block_max)
        weights = jnp.exp(scores - m_new)
        if allowed is not None:
            weights = jnp.where(allowed, weights, 0.0)
        shrink = jnp.exp(m_old - m_new)
        l_new = l_old * shrink + jnp.sum(weights, axis=1, keepdims=True)
        pv = jnp.dot(weights.astype(jnp.bfloat16), kv, preferred_element_type=jnp.float32)
        lane = lax.broadcasted_iota(jnp.int32, (rows, width), 1)
        acc = state * shrink + pv
        out_ref[...] = jnp.where(
            lane >= HD, acc, jnp.where(lane == 0, m_new, jnp.where(lane == 1, l_new, 0.0))
        )

    @pl.when(none_allowed)
    def _():
        out_ref[...] = s_ref[...]

    @pl.when(all_allowed & jnp.logical_not(none_allowed))
    def _():
        update(None)

    @pl.when(jnp.logical_not(all_allowed) & jnp.logical_not(none_allowed))
    def _():
        kpos = kstart + lax.broadcasted_iota(jnp.int32, (1, keys), 1)
        kpos = jnp.where((valid_ref[...] > 0) | (check_valid == 0), kpos, FAR)
        tpos = qstart + lax.broadcasted_iota(jnp.int32, (rows, 1), 0)
        update((kpos >= seg_ref[...]) & (kpos <= tpos))


def attend_step(info, valid_row, seg_col, q_hm, kv_hm, state):
    heads, rows, _ = q_hm.shape
    keys = kv_hm.shape[1]
    width = kv_hm.shape[2]
    grid_spec = pltpu.PrefetchScalarGridSpec(
        num_scalar_prefetch=1,
        grid=(heads,),
        in_specs=[
            pl.BlockSpec((1, keys), lambda h, info: (0, 0)),
            pl.BlockSpec((rows, 1), lambda h, info: (0, 0)),
            pl.BlockSpec((None, rows, HD), lambda h, info: (h, 0, 0)),
            pl.BlockSpec((None, keys, width), lambda h, info: (h, 0, 0)),
            pl.BlockSpec((None, rows, width), lambda h, info: (h, 0, 0)),
        ],
        out_specs=pl.BlockSpec((None, rows, width), lambda h, info: (h, 0, 0)),
    )
    flops = heads * rows * keys * (2 * HD + 2 * width)
    return pl.pallas_call(
        _step_kernel,
        grid_spec=grid_spec,
        out_shape=jax.ShapeDtypeStruct(state.shape, jnp.float32),
        input_output_aliases={5: 0},
        cost_estimate=pl.CostEstimate(
            flops=flops,
            transcendentals=heads * rows * keys,
            bytes_accessed=q_hm.size * 2 + kv_hm.size * 2 + state.size * 8,
        ),
    )(info, valid_row, seg_col, q_hm, kv_hm, state)


def passed_along(x, axis, by):
    count = lax.axis_size(axis)
    pairs = [(i, i + by) for i in range(count) if 0 <= i + by < count]
    return lax.ppermute(x, axis, pairs)


def rotate(inputs, positions):
    half_dim = inputs.shape[-1] // 2
    frequency = THETA ** (-2.0 * jnp.arange(half_dim, dtype=jnp.float32) / inputs.shape[-1])
    angles = positions.astype(jnp.float32)[:, None] * frequency[None, :]
    cosine = jnp.cos(angles)[:, None, :]
    sine_part = jnp.sin(angles)[:, None, :]
    front_half = inputs[..., :half_dim]
    back_half = inputs[..., half_dim:]
    return jnp.concatenate(
        [front_half * cosine - back_half * sine_part, back_half * cosine + front_half * sine_part],
        axis=-1,
    )


def body(
    residual,
    norm_gain,
    query_weight,
    key_weight,
    value_weight,
    out_weight,
    segment_start,
    token_valid,
    page_slot,
):
    row_count = residual.shape[0]
    local_heads = query_weight.shape[1] // HD
    seq_rank = lax.axis_index("seq")
    seq_count = lax.axis_size("seq")
    reach_dev = min(SPAN, seq_count // 2)
    half = seq_count // 2
    chain = [(i, i + 1) for i in range(seq_count - 1)]
    inner = [p for p in chain if p != (half - 1, half)]
    first_block = segment_start[0] // row_count
    cross_here = jnp.clip(seq_rank - first_block, 0, reach_dev).astype(jnp.int32)
    cross_steps = lax.psum(jnp.where(seq_rank == half, cross_here, 0), "seq")

    cross_steps = jnp.maximum(cross_steps, 1)
    residual, cross_steps = lax.optimization_barrier((residual, cross_steps))
    gathered = lax.all_gather(residual, "tp", axis=1, tiled=True)
    widened = gathered.astype(jnp.float32)
    mean_sq = jnp.mean(widened * widened, axis=1, keepdims=True)
    normed = (widened * lax.rsqrt(mean_sq + EPS) * norm_gain[None, :]).astype(jnp.bfloat16)
    seq_rank = lax.axis_index("seq")
    first_row = seq_rank * row_count
    places = first_row + jnp.arange(row_count, dtype=jnp.int32)
    offsets = places - segment_start
    queries = jnp.dot(normed, query_weight, preferred_element_type=jnp.float32).reshape(
        row_count, local_heads, HD
    )
    queries = rotate(queries, offsets).astype(jnp.bfloat16)
    key_rot = jnp.dot(normed, key_weight, preferred_element_type=jnp.float32).reshape(
        row_count, local_heads, HD
    )
    key_rot = rotate(key_rot, offsets).astype(jnp.bfloat16)
    values = (
        jnp.dot(normed, value_weight, preferred_element_type=jnp.float32)
        .reshape(row_count, local_heads, HD)
        .astype(jnp.bfloat16)
    )
    packed = jnp.concatenate([key_rot[:, :, None, :], values[:, :, None, :]], axis=2).reshape(
        row_count, local_heads * 2 * HD
    )
    packed = jnp.where(token_valid[:, None] > 0, packed, jnp.zeros_like(packed))

    out_cols = lax.all_to_all(out_weight, "tp", 1, 0, tiled=True)
    prev_slot = passed_along(page_slot, "seq", 1)

    q_hm = jnp.transpose(queries, (1, 0, 2))
    kv_hm = jnp.transpose(packed.reshape(row_count, local_heads, 2 * HD), (1, 0, 2))
    seg_col = segment_start[:, None]
    valid_row = token_valid[None, :]
    seg_last = segment_start[row_count - 1]

    def absorb(state, incoming, step):
        info = jnp.stack(
            [first_row - step * row_count, first_row, (jnp.asarray(step) == 0).astype(jnp.int32), seg_last]
        ).astype(jnp.int32)
        return attend_step(info, valid_row, seg_col, q_hm, incoming, state)

    lane = jnp.arange(2 * HD, dtype=jnp.int32)
    initial = jnp.broadcast_to(
        jnp.where(lane == 0, -1e30, 0.0).astype(jnp.float32), (local_heads, row_count, 2 * HD)
    )

    prev_block = lax.ppermute(kv_hm, "seq", chain)
    carried = absorb(initial, kv_hm, 0)

    def step_with(pairs):
        def advance(step_index, carry_in):
            held, state = carry_in
            sent = lax.ppermute(held, "seq", pairs)
            state = absorb(state, held, step_index)
            return (sent, state)

        return advance

    held, carried = lax.fori_loop(1, cross_steps, step_with(chain), (prev_block, carried))
    held, carried = lax.fori_loop(cross_steps, reach_dev, step_with(inner), (held, carried))
    carried = absorb(carried, held, reach_dev)
    attended = (
        jnp.transpose(carried[:, :, HD:] / carried[:, :, 1:2], (1, 0, 2))
        .astype(jnp.bfloat16)
        .reshape(row_count, local_heads * HD)
    )

    tiles = page_slot.shape[0]
    slot_count = 2 * tiles
    base_slot = seq_rank * slot_count
    has_prev = seq_rank > 0
    cand_slot = jnp.concatenate([page_slot, jnp.where(has_prev, prev_slot, -1)]) - base_slot
    cand_pages = jnp.concatenate(
        [packed.reshape(tiles, PAGE, -1), jnp.transpose(prev_block, (1, 0, 2)).reshape(tiles, PAGE, -1)],
        axis=0,
    )
    match = cand_slot[None, :] == jnp.arange(slot_count, dtype=jnp.int32)[:, None]
    pick = jnp.argmax(match.astype(jnp.int32), axis=1)
    found = jnp.any(match, axis=1)
    cache_pages = jnp.where(found[:, None, None], cand_pages[pick], jnp.zeros_like(cand_pages[:1]))

    attended_all = lax.all_gather(attended, "tp", axis=1, tiled=True)
    projected = jnp.dot(attended_all, out_cols, preferred_element_type=jnp.float32)
    hidden = (residual.astype(jnp.float32) + projected).astype(jnp.bfloat16)
    return (hidden, cache_pages)


def solution(mesh):
    return jax.shard_map(
        body,
        mesh=mesh,
        in_specs=(
            P("seq", "tp"),
            P(),
            P(None, "tp"),
            P(None, "tp"),
            P(None, "tp"),
            P("tp", None),
            P("seq"),
            P("seq"),
            P("seq"),
        ),
        out_specs=(P("seq", "tp"), P("seq", None, "tp")),
        check_vma=False,
    )
```

```python
import jax
import jax.numpy as jnp
from jax import lax
from jax.experimental import pallas as pl
from jax.experimental.pallas import tpu as pltpu
from jax.sharding import PartitionSpec as P

HD = 64
PAGE = 128
SPAN = 16


THETA = 130000.0
EPS = 1e-05
SCALE = HD ** (-0.5)
FAR = 1 << 30


def _step_kernel(step_ref, meta_ref, valid_ref, seg_ref, q_ref, kv_a_ref, kv_b_ref, s_ref, out_ref):
    rows, width = out_ref.shape
    keys = kv_a_ref.shape[0]
    step = step_ref[0]
    qstart = meta_ref[0]
    check_valid = jnp.where(step == 0, meta_ref[1], 0)
    seg_last = meta_ref[2]
    kstart = qstart - step * keys
    seg_first = seg_ref[0, 0]
    none_allowed = kstart + keys - 1 < seg_first
    all_allowed = (seg_last <= kstart) & (kstart + keys - 1 <= qstart) & (check_valid == 0)
    first_half = pl.program_id(0) < 2

    def update(allowed):
        q = q_ref[...]
        kv = jnp.where(first_half, kv_a_ref[...], kv_b_ref[...])
        scores = lax.dot_general(
            q, kv[:, :HD], (((1,), (1,)), ((), ())), preferred_element_type=jnp.float32
        ) * SCALE
        state = s_ref[...]
        m_old = state[:, 0:1]
        l_old = state[:, 1:2]
        if allowed is None:
            block_max = jnp.max(scores, axis=1, keepdims=True)
        else:
            block_max = jnp.max(jnp.where(allowed, scores, -1e30), axis=1, keepdims=True)
        m_new = jnp.maximum(m_old, block_max)
        weights = jnp.exp(scores - m_new)
        if allowed is not None:
            weights = jnp.where(allowed, weights, 0.0)
        shrink = jnp.exp(m_old - m_new)
        l_new = l_old * shrink + jnp.sum(weights, axis=1, keepdims=True)
        pv = jnp.dot(weights.astype(jnp.bfloat16), kv, preferred_element_type=jnp.float32)
        lane = lax.broadcasted_iota(jnp.int32, (rows, width), 1)
        acc = state * shrink + pv
        out_ref[...] = jnp.where(
            lane >= HD, acc, jnp.where(lane == 0, m_new, jnp.where(lane == 1, l_new, 0.0))
        )

    @pl.when(none_allowed)
    def _():
        out_ref[...] = s_ref[...]

    @pl.when(all_allowed & jnp.logical_not(none_allowed))
    def _():
        update(None)

    @pl.when(jnp.logical_not(all_allowed) & jnp.logical_not(none_allowed))
    def _():
        kpos = kstart + lax.broadcasted_iota(jnp.int32, (1, keys), 1)
        kpos = jnp.where((valid_ref[...] > 0) | (check_valid == 0), kpos, FAR)
        tpos = qstart + lax.broadcasted_iota(jnp.int32, (rows, 1), 0)
        update((kpos >= seg_ref[...]) & (kpos <= tpos))


def attend_step(step, meta, valid_row, seg_col, q_hm, kv_a, kv_b, state):
    heads, rows, _ = q_hm.shape
    part = kv_a.shape[0]
    keys = kv_a.shape[1]
    width = kv_a.shape[2]
    grid_spec = pltpu.PrefetchScalarGridSpec(
        num_scalar_prefetch=2,
        grid=(heads,),
        in_specs=[
            pl.BlockSpec((1, keys), lambda h, s, m: (0, 0)),
            pl.BlockSpec((rows, 1), lambda h, s, m: (0, 0)),
            pl.BlockSpec((None, rows, HD), lambda h, s, m: (h, 0, 0)),
            pl.BlockSpec((None, keys, width), lambda h, s, m: (h % part, 0, 0)),
            pl.BlockSpec((None, keys, width), lambda h, s, m: (h % part, 0, 0)),
            pl.BlockSpec((None, rows, width), lambda h, s, m: (h, 0, 0)),
        ],
        out_specs=pl.BlockSpec((None, rows, width), lambda h, s, m: (h, 0, 0)),
    )
    flops = heads * rows * keys * (2 * HD + 2 * width)
    return pl.pallas_call(
        _step_kernel,
        grid_spec=grid_spec,
        out_shape=jax.ShapeDtypeStruct(state.shape, jnp.float32),
        input_output_aliases={7: 0},
        cost_estimate=pl.CostEstimate(
            flops=flops,
            transcendentals=heads * rows * keys,
            bytes_accessed=q_hm.size * 2 + 2 * (kv_a.size + kv_b.size) * 2 + state.size * 8,
        ),
    )(step, meta, valid_row, seg_col, q_hm, kv_a, kv_b, state)


def passed_along(x, axis, by):
    count = lax.axis_size(axis)
    pairs = [(i, i + by) for i in range(count) if 0 <= i + by < count]
    return lax.ppermute(x, axis, pairs)


def rotate(inputs, positions):
    half_dim = inputs.shape[-1] // 2
    frequency = THETA ** (-2.0 * jnp.arange(half_dim, dtype=jnp.float32) / inputs.shape[-1])
    angles = positions.astype(jnp.float32)[:, None] * frequency[None, :]
    cosine = jnp.cos(angles)[:, None, :]
    sine_part = jnp.sin(angles)[:, None, :]
    front_half = inputs[..., :half_dim]
    back_half = inputs[..., half_dim:]
    return jnp.concatenate(
        [front_half * cosine - back_half * sine_part, back_half * cosine + front_half * sine_part],
        axis=-1,
    )


def body(
    residual,
    norm_gain,
    query_weight,
    key_weight,
    value_weight,
    out_weight,
    segment_start,
    token_valid,
    page_slot,
):
    row_count = residual.shape[0]
    local_heads = query_weight.shape[1] // HD
    seq_rank = lax.axis_index("seq")
    seq_count = lax.axis_size("seq")
    reach_dev = min(SPAN, seq_count // 2)
    half = seq_count // 2
    chain = [(i, i + 1) for i in range(seq_count - 1)]
    inner = [p for p in chain if p != (half - 1, half)]
    first_block = segment_start[0] // row_count
    cross_here = jnp.clip(seq_rank - first_block, 0, reach_dev).astype(jnp.int32)
    cross_steps = lax.psum(jnp.where(seq_rank == half, cross_here, 0), "seq")

    cross_steps = jnp.maximum(cross_steps, 1)
    residual, cross_steps = lax.optimization_barrier((residual, cross_steps))
    gathered = lax.all_gather(residual, "tp", axis=1, tiled=True)
    widened = gathered.astype(jnp.float32)
    mean_sq = jnp.mean(widened * widened, axis=1, keepdims=True)
    normed = (widened * lax.rsqrt(mean_sq + EPS) * norm_gain[None, :]).astype(jnp.bfloat16)
    seq_rank = lax.axis_index("seq")
    first_row = seq_rank * row_count
    places = first_row + jnp.arange(row_count, dtype=jnp.int32)
    offsets = places - segment_start
    queries = jnp.dot(normed, query_weight, preferred_element_type=jnp.float32).reshape(
        row_count, local_heads, HD
    )
    queries = rotate(queries, offsets).astype(jnp.bfloat16)
    key_rot = jnp.dot(normed, key_weight, preferred_element_type=jnp.float32).reshape(
        row_count, local_heads, HD
    )
    key_rot = rotate(key_rot, offsets).astype(jnp.bfloat16)
    values = (
        jnp.dot(normed, value_weight, preferred_element_type=jnp.float32)
        .reshape(row_count, local_heads, HD)
        .astype(jnp.bfloat16)
    )
    packed = jnp.concatenate([key_rot[:, :, None, :], values[:, :, None, :]], axis=2).reshape(
        row_count, local_heads * 2 * HD
    )
    packed = jnp.where(token_valid[:, None] > 0, packed, jnp.zeros_like(packed))

    out_cols = lax.all_to_all(out_weight, "tp", 1, 0, tiled=True)
    prev_slot = passed_along(page_slot, "seq", 1)

    q_hm = jnp.transpose(queries, (1, 0, 2))
    kv_hm = jnp.transpose(packed.reshape(row_count, local_heads, 2 * HD), (1, 0, 2))
    seg_col = segment_start[:, None]
    valid_row = token_valid[None, :]
    seg_last = segment_start[row_count - 1]

    meta = jnp.stack([first_row, 1, seg_last]).astype(jnp.int32)
    split = local_heads // 2

    def absorb(state, incoming, step):
        step_arr = jnp.asarray(step, jnp.int32).reshape(1)
        return attend_step(step_arr, meta, valid_row, seg_col, q_hm, incoming[0], incoming[1], state)

    lane = jnp.arange(2 * HD, dtype=jnp.int32)
    initial = jnp.broadcast_to(
        jnp.where(lane == 0, -1e30, 0.0).astype(jnp.float32), (local_heads, row_count, 2 * HD)
    )

    own = (kv_hm[:split], kv_hm[split:])
    prev_block = tuple(lax.ppermute(part, "seq", chain) for part in own)
    carried = absorb(initial, own, 0)

    def step_with(pairs):
        def advance(step_index, carry_in):
            held, state = carry_in
            sent = tuple(lax.ppermute(part, "seq", pairs) for part in held)
            state = absorb(state, held, step_index)
            return (sent, state)

        return advance

    held, carried = lax.fori_loop(1, cross_steps, step_with(chain), (prev_block, carried))
    held, carried = lax.fori_loop(cross_steps, reach_dev, step_with(inner), (held, carried))
    carried = absorb(carried, held, reach_dev)
    attended = (
        jnp.transpose(carried[:, :, HD:] / carried[:, :, 1:2], (1, 0, 2))
        .astype(jnp.bfloat16)
        .reshape(row_count, local_heads * HD)
    )

    tiles = page_slot.shape[0]
    slot_count = 2 * tiles
    base_slot = seq_rank * slot_count
    has_prev = seq_rank > 0
    cand_slot = jnp.concatenate([page_slot, jnp.where(has_prev, prev_slot, -1)]) - base_slot
    cand_pages = jnp.concatenate(
        [packed.reshape(tiles, PAGE, -1), jnp.transpose(jnp.concatenate(prev_block, axis=0), (1, 0, 2)).reshape(tiles, PAGE, -1)],
        axis=0,
    )
    match = cand_slot[None, :] == jnp.arange(slot_count, dtype=jnp.int32)[:, None]
    pick = jnp.argmax(match.astype(jnp.int32), axis=1)
    found = jnp.any(match, axis=1)
    cache_pages = jnp.where(found[:, None, None], cand_pages[pick], jnp.zeros_like(cand_pages[:1]))

    attended_all = lax.all_gather(attended, "tp", axis=1, tiled=True)
    projected = jnp.dot(attended_all, out_cols, preferred_element_type=jnp.float32)
    hidden = (residual.astype(jnp.float32) + projected).astype(jnp.bfloat16)
    return (hidden, cache_pages)


def solution(mesh):
    return jax.shard_map(
        body,
        mesh=mesh,
        in_specs=(
            P("seq", "tp"),
            P(),
            P(None, "tp"),
            P(None, "tp"),
            P(None, "tp"),
            P("tp", None),
            P("seq"),
            P("seq"),
            P("seq"),
        ),
        out_specs=(P("seq", "tp"), P("seq", None, "tp")),
        check_vma=False,
    )
```

```python
import jax
import jax.numpy as jnp
from jax import lax
from jax.experimental import pallas as pl
from jax.experimental.pallas import tpu as pltpu
from jax.sharding import PartitionSpec as P

HD = 64
PAGE = 128
SPAN = 16


THETA = 130000.0
EPS = 1e-05
SCALE = HD ** (-0.5)
FAR = 1 << 30


def _step_kernel(step_ref, meta_ref, valid_ref, seg_ref, q_ref, kv_a_ref, kv_b_ref, s_ref, out_ref):
    rows, width = out_ref.shape
    keys = kv_a_ref.shape[0]
    step = step_ref[0]
    qstart = meta_ref[0]
    check_valid = jnp.where(step == 0, meta_ref[1], 0)
    seg_last = meta_ref[2]
    kstart = qstart - step * keys
    seg_first = seg_ref[0, 0]
    none_allowed = kstart + keys - 1 < seg_first
    all_allowed = (seg_last <= kstart) & (kstart + keys - 1 <= qstart) & (check_valid == 0)
    first_half = pl.program_id(0) < 2

    def update(allowed):
        q = q_ref[...]
        kv = jnp.where(first_half, kv_a_ref[...], kv_b_ref[...])
        scores = lax.dot_general(
            q, kv[:, :HD], (((1,), (1,)), ((), ())), preferred_element_type=jnp.float32
        ) * SCALE
        state = s_ref[...]
        m_old = state[:, 0:1]
        l_old = state[:, 1:2]
        if allowed is None:
            block_max = jnp.max(scores, axis=1, keepdims=True)
        else:
            block_max = jnp.max(jnp.where(allowed, scores, -1e30), axis=1, keepdims=True)
        m_new = jnp.maximum(m_old, block_max)
        weights = jnp.exp(scores - m_new)
        if allowed is not None:
            weights = jnp.where(allowed, weights, 0.0)
        shrink = jnp.exp(m_old - m_new)
        l_new = l_old * shrink + jnp.sum(weights, axis=1, keepdims=True)
        pv = jnp.dot(weights.astype(jnp.bfloat16), kv, preferred_element_type=jnp.float32)
        lane = lax.broadcasted_iota(jnp.int32, (rows, width), 1)
        acc = state * shrink + pv
        out_ref[...] = jnp.where(
            lane >= HD, acc, jnp.where(lane == 0, m_new, jnp.where(lane == 1, l_new, 0.0))
        )

    @pl.when(none_allowed)
    def _():
        out_ref[...] = s_ref[...]

    @pl.when(all_allowed & jnp.logical_not(none_allowed))
    def _():
        update(None)

    @pl.when(jnp.logical_not(all_allowed) & jnp.logical_not(none_allowed))
    def _():
        kpos = kstart + lax.broadcasted_iota(jnp.int32, (1, keys), 1)
        kpos = jnp.where((valid_ref[...] > 0) | (check_valid == 0), kpos, FAR)
        tpos = qstart + lax.broadcasted_iota(jnp.int32, (rows, 1), 0)
        update((kpos >= seg_ref[...]) & (kpos <= tpos))


def attend_step(step, meta, valid_row, seg_col, q_hm, kv_a, kv_b, state):
    heads, rows, _ = q_hm.shape
    part = kv_a.shape[0]
    keys = kv_a.shape[1]
    width = kv_a.shape[2]
    grid_spec = pltpu.PrefetchScalarGridSpec(
        num_scalar_prefetch=2,
        grid=(heads,),
        in_specs=[
            pl.BlockSpec((1, keys), lambda h, s, m: (0, 0)),
            pl.BlockSpec((rows, 1), lambda h, s, m: (0, 0)),
            pl.BlockSpec((None, rows, HD), lambda h, s, m: (h, 0, 0)),
            pl.BlockSpec((None, keys, width), lambda h, s, m: (h % part, 0, 0)),
            pl.BlockSpec((None, keys, width), lambda h, s, m: (h % part, 0, 0)),
            pl.BlockSpec((None, rows, width), lambda h, s, m: (h, 0, 0)),
        ],
        out_specs=pl.BlockSpec((None, rows, width), lambda h, s, m: (h, 0, 0)),
    )
    flops = heads * rows * keys * (2 * HD + 2 * width)
    return pl.pallas_call(
        _step_kernel,
        grid_spec=grid_spec,
        out_shape=jax.ShapeDtypeStruct(state.shape, jnp.float32),
        input_output_aliases={7: 0},
        cost_estimate=pl.CostEstimate(
            flops=flops,
            transcendentals=heads * rows * keys,
            bytes_accessed=q_hm.size * 2 + 2 * (kv_a.size + kv_b.size) * 2 + state.size * 8,
        ),
    )(step, meta, valid_row, seg_col, q_hm, kv_a, kv_b, state)


def passed_along(x, axis, by):
    count = lax.axis_size(axis)
    pairs = [(i, i + by) for i in range(count) if 0 <= i + by < count]
    return lax.ppermute(x, axis, pairs)


def rotate(inputs, positions):
    half_dim = inputs.shape[-1] // 2
    frequency = THETA ** (-2.0 * jnp.arange(half_dim, dtype=jnp.float32) / inputs.shape[-1])
    angles = positions.astype(jnp.float32)[:, None] * frequency[None, :]
    cosine = jnp.cos(angles)[:, None, :]
    sine_part = jnp.sin(angles)[:, None, :]
    front_half = inputs[..., :half_dim]
    back_half = inputs[..., half_dim:]
    return jnp.concatenate(
        [front_half * cosine - back_half * sine_part, back_half * cosine + front_half * sine_part],
        axis=-1,
    )


def body(
    residual,
    norm_gain,
    query_weight,
    key_weight,
    value_weight,
    out_weight,
    segment_start,
    token_valid,
    page_slot,
):
    row_count = residual.shape[0]
    local_heads = query_weight.shape[1] // HD
    seq_rank = lax.axis_index("seq")
    seq_count = lax.axis_size("seq")
    reach_dev = min(SPAN, seq_count // 2)
    half = seq_count // 2
    chain = [(i, i + 1) for i in range(seq_count - 1)]
    inner = [p for p in chain if p != (half - 1, half)]
    first_block = segment_start[0] // row_count
    cross_here = jnp.clip(seq_rank - first_block, 0, reach_dev).astype(jnp.int32)
    told = jnp.broadcast_to(jnp.where(seq_rank == half, cross_here, 0), (seq_count,))
    cross_steps = jnp.sum(lax.all_to_all(told, "seq", 0, 0, tiled=True))
    cross_steps = jnp.maximum(cross_steps, 1)
    gathered = lax.all_gather(residual, "tp", axis=1, tiled=True)
    widened = gathered.astype(jnp.float32)
    mean_sq = jnp.mean(widened * widened, axis=1, keepdims=True)
    normed = (widened * lax.rsqrt(mean_sq + EPS) * norm_gain[None, :]).astype(jnp.bfloat16)
    seq_rank = lax.axis_index("seq")
    first_row = seq_rank * row_count
    places = first_row + jnp.arange(row_count, dtype=jnp.int32)
    offsets = places - segment_start
    queries = jnp.dot(normed, query_weight, preferred_element_type=jnp.float32).reshape(
        row_count, local_heads, HD
    )
    queries = rotate(queries, offsets).astype(jnp.bfloat16)
    key_rot = jnp.dot(normed, key_weight, preferred_element_type=jnp.float32).reshape(
        row_count, local_heads, HD
    )
    key_rot = rotate(key_rot, offsets).astype(jnp.bfloat16)
    values = (
        jnp.dot(normed, value_weight, preferred_element_type=jnp.float32)
        .reshape(row_count, local_heads, HD)
        .astype(jnp.bfloat16)
    )
    packed = jnp.concatenate([key_rot[:, :, None, :], values[:, :, None, :]], axis=2).reshape(
        row_count, local_heads * 2 * HD
    )
    packed = jnp.where(token_valid[:, None] > 0, packed, jnp.zeros_like(packed))

    out_cols = lax.all_to_all(out_weight, "tp", 1, 0, tiled=True)
    prev_slot = passed_along(page_slot, "seq", 1)

    q_hm = jnp.transpose(queries, (1, 0, 2))
    kv_hm = jnp.transpose(packed.reshape(row_count, local_heads, 2 * HD), (1, 0, 2))
    seg_col = segment_start[:, None]
    valid_row = token_valid[None, :]
    seg_last = segment_start[row_count - 1]

    meta = jnp.stack([first_row, 1, seg_last]).astype(jnp.int32)
    split = local_heads // 2

    def absorb(state, incoming, step):
        step_arr = jnp.asarray(step, jnp.int32).reshape(1)
        return attend_step(step_arr, meta, valid_row, seg_col, q_hm, incoming[0], incoming[1], state)

    lane = jnp.arange(2 * HD, dtype=jnp.int32)
    initial = jnp.broadcast_to(
        jnp.where(lane == 0, -1e30, 0.0).astype(jnp.float32), (local_heads, row_count, 2 * HD)
    )

    own = (kv_hm[:split], kv_hm[split:])
    prev_block = tuple(lax.ppermute(part, "seq", chain) for part in own)
    carried = absorb(initial, own, 0)

    def step_with(pairs):
        def advance(step_index, carry_in):
            held, state = carry_in
            sent = tuple(lax.ppermute(part, "seq", pairs) for part in held)
            state = absorb(state, held, step_index)
            return (sent, state)

        return advance

    held, carried = lax.fori_loop(1, cross_steps, step_with(chain), (prev_block, carried))
    held, carried = lax.fori_loop(cross_steps, reach_dev, step_with(inner), (held, carried))
    carried = absorb(carried, held, reach_dev)
    attended = (
        jnp.transpose(carried[:, :, HD:] / carried[:, :, 1:2], (1, 0, 2))
        .astype(jnp.bfloat16)
        .reshape(row_count, local_heads * HD)
    )

    tiles = page_slot.shape[0]
    slot_count = 2 * tiles
    base_slot = seq_rank * slot_count
    has_prev = seq_rank > 0
    cand_slot = jnp.concatenate([page_slot, jnp.where(has_prev, prev_slot, -1)]) - base_slot
    cand_pages = jnp.concatenate(
        [packed.reshape(tiles, PAGE, -1), jnp.transpose(jnp.concatenate(prev_block, axis=0), (1, 0, 2)).reshape(tiles, PAGE, -1)],
        axis=0,
    )
    match = cand_slot[None, :] == jnp.arange(slot_count, dtype=jnp.int32)[:, None]
    pick = jnp.argmax(match.astype(jnp.int32), axis=1)
    found = jnp.any(match, axis=1)
    cache_pages = jnp.where(found[:, None, None], cand_pages[pick], jnp.zeros_like(cand_pages[:1]))

    attended_all = lax.all_gather(attended, "tp", axis=1, tiled=True)
    projected = jnp.dot(attended_all, out_cols, preferred_element_type=jnp.float32)
    hidden = (residual.astype(jnp.float32) + projected).astype(jnp.bfloat16)
    return (hidden, cache_pages)


def solution(mesh):
    return jax.shard_map(
        body,
        mesh=mesh,
        in_specs=(
            P("seq", "tp"),
            P(),
            P(None, "tp"),
            P(None, "tp"),
            P(None, "tp"),
            P("tp", None),
            P("seq"),
            P("seq"),
            P("seq"),
        ),
        out_specs=(P("seq", "tp"), P("seq", None, "tp")),
        check_vma=False,
    )
```

```python
import jax
import jax.numpy as jnp
from jax import lax
from jax.experimental import pallas as pl
from jax.experimental.pallas import tpu as pltpu
from jax.sharding import PartitionSpec as P

HD = 64
PAGE = 128
SPAN = 16


THETA = 130000.0
EPS = 1e-05
SCALE = HD ** (-0.5)
FAR = 1 << 30


def _step_kernel(step_ref, meta_ref, valid_ref, seg_ref, q_ref, kv_a_ref, kv_b_ref, s_ref, out_ref):
    rows, width = out_ref.shape
    keys = kv_a_ref.shape[0]
    step = step_ref[0]
    qstart = meta_ref[0]
    check_valid = jnp.where(step == 0, meta_ref[1], 0)
    seg_last = meta_ref[2]
    kstart = qstart - step * keys
    seg_first = seg_ref[0, 0]
    none_allowed = kstart + keys - 1 < seg_first
    all_allowed = (seg_last <= kstart) & (kstart + keys - 1 <= qstart) & (check_valid == 0)
    first_half = pl.program_id(0) < 2

    def update(allowed):
        q = q_ref[...]
        kv = jnp.where(first_half, kv_a_ref[...], kv_b_ref[...])
        scores = lax.dot_general(
            q, kv[:, :HD], (((1,), (1,)), ((), ())), preferred_element_type=jnp.float32
        ) * SCALE
        state = s_ref[...]
        m_old = state[:, 0:1]
        l_old = state[:, 1:2]
        if allowed is None:
            block_max = jnp.max(scores, axis=1, keepdims=True)
        else:
            block_max = jnp.max(jnp.where(allowed, scores, -1e30), axis=1, keepdims=True)
        m_new = jnp.maximum(m_old, block_max)
        weights = jnp.exp(scores - m_new)
        if allowed is not None:
            weights = jnp.where(allowed, weights, 0.0)
        shrink = jnp.exp(m_old - m_new)
        l_new = l_old * shrink + jnp.sum(weights, axis=1, keepdims=True)
        pv = jnp.dot(weights.astype(jnp.bfloat16), kv, preferred_element_type=jnp.float32)
        lane = lax.broadcasted_iota(jnp.int32, (rows, width), 1)
        acc = state * shrink + pv
        out_ref[...] = jnp.where(
            lane >= HD, acc, jnp.where(lane == 0, m_new, jnp.where(lane == 1, l_new, 0.0))
        )

    @pl.when(none_allowed)
    def _():
        out_ref[...] = s_ref[...]

    @pl.when(all_allowed & jnp.logical_not(none_allowed))
    def _():
        update(None)

    @pl.when(jnp.logical_not(all_allowed) & jnp.logical_not(none_allowed))
    def _():
        kpos = kstart + lax.broadcasted_iota(jnp.int32, (1, keys), 1)
        kpos = jnp.where((valid_ref[...] > 0) | (check_valid == 0), kpos, FAR)
        tpos = qstart + lax.broadcasted_iota(jnp.int32, (rows, 1), 0)
        update((kpos >= seg_ref[...]) & (kpos <= tpos))


def attend_step(step, meta, valid_row, seg_col, q_hm, kv_a, kv_b, state):
    heads, rows, _ = q_hm.shape
    part = kv_a.shape[0]
    keys = kv_a.shape[1]
    width = kv_a.shape[2]
    grid_spec = pltpu.PrefetchScalarGridSpec(
        num_scalar_prefetch=2,
        grid=(heads,),
        in_specs=[
            pl.BlockSpec((1, keys), lambda h, s, m: (0, 0)),
            pl.BlockSpec((rows, 1), lambda h, s, m: (0, 0)),
            pl.BlockSpec((None, rows, HD), lambda h, s, m: (h, 0, 0)),
            pl.BlockSpec((None, keys, width), lambda h, s, m: (h % part, 0, 0)),
            pl.BlockSpec((None, keys, width), lambda h, s, m: (h % part, 0, 0)),
            pl.BlockSpec((None, rows, width), lambda h, s, m: (h, 0, 0)),
        ],
        out_specs=pl.BlockSpec((None, rows, width), lambda h, s, m: (h, 0, 0)),
    )
    flops = heads * rows * keys * (2 * HD + 2 * width)
    return pl.pallas_call(
        _step_kernel,
        grid_spec=grid_spec,
        out_shape=jax.ShapeDtypeStruct(state.shape, jnp.float32),
        input_output_aliases={7: 0},
        cost_estimate=pl.CostEstimate(
            flops=flops,
            transcendentals=heads * rows * keys,
            bytes_accessed=q_hm.size * 2 + 2 * (kv_a.size + kv_b.size) * 2 + state.size * 8,
        ),
    )(step, meta, valid_row, seg_col, q_hm, kv_a, kv_b, state)


def tp_gather(x, count):
    copies = jnp.broadcast_to(x[None], (count,) + x.shape)
    got = lax.all_to_all(copies, "tp", 0, 0, tiled=True)
    return jnp.transpose(got, (1, 0, 2)).reshape(x.shape[0], count * x.shape[1])


def passed_along(x, axis, by):
    count = lax.axis_size(axis)
    pairs = [(i, i + by) for i in range(count) if 0 <= i + by < count]
    return lax.ppermute(x, axis, pairs)


def rotate(inputs, positions):
    half_dim = inputs.shape[-1] // 2
    frequency = THETA ** (-2.0 * jnp.arange(half_dim, dtype=jnp.float32) / inputs.shape[-1])
    angles = positions.astype(jnp.float32)[:, None] * frequency[None, :]
    cosine = jnp.cos(angles)[:, None, :]
    sine_part = jnp.sin(angles)[:, None, :]
    front_half = inputs[..., :half_dim]
    back_half = inputs[..., half_dim:]
    return jnp.concatenate(
        [front_half * cosine - back_half * sine_part, back_half * cosine + front_half * sine_part],
        axis=-1,
    )


def body(
    residual,
    norm_gain,
    query_weight,
    key_weight,
    value_weight,
    out_weight,
    segment_start,
    token_valid,
    page_slot,
):
    row_count = residual.shape[0]
    local_heads = query_weight.shape[1] // HD
    seq_rank = lax.axis_index("seq")
    seq_count = lax.axis_size("seq")
    reach_dev = min(SPAN, seq_count // 2)
    half = seq_count // 2
    chain = [(i, i + 1) for i in range(seq_count - 1)]
    inner = [p for p in chain if p != (half - 1, half)]
    first_block = segment_start[0] // row_count
    cross_here = jnp.clip(seq_rank - first_block, 0, reach_dev).astype(jnp.int32)
    told = jnp.broadcast_to(jnp.where(seq_rank == half, cross_here, 0), (seq_count,))
    cross_steps = jnp.sum(lax.all_to_all(told, "seq", 0, 0, tiled=True))
    cross_steps = jnp.maximum(cross_steps, 1)
    tp_count = lax.axis_size("tp")
    gathered = tp_gather(residual, tp_count)
    widened = gathered.astype(jnp.float32)
    mean_sq = jnp.mean(widened * widened, axis=1, keepdims=True)
    normed = (widened * lax.rsqrt(mean_sq + EPS) * norm_gain[None, :]).astype(jnp.bfloat16)
    seq_rank = lax.axis_index("seq")
    first_row = seq_rank * row_count
    places = first_row + jnp.arange(row_count, dtype=jnp.int32)
    offsets = places - segment_start
    queries = jnp.dot(normed, query_weight, preferred_element_type=jnp.float32).reshape(
        row_count, local_heads, HD
    )
    queries = rotate(queries, offsets).astype(jnp.bfloat16)
    key_rot = jnp.dot(normed, key_weight, preferred_element_type=jnp.float32).reshape(
        row_count, local_heads, HD
    )
    key_rot = rotate(key_rot, offsets).astype(jnp.bfloat16)
    values = (
        jnp.dot(normed, value_weight, preferred_element_type=jnp.float32)
        .reshape(row_count, local_heads, HD)
        .astype(jnp.bfloat16)
    )
    packed = jnp.concatenate([key_rot[:, :, None, :], values[:, :, None, :]], axis=2).reshape(
        row_count, local_heads * 2 * HD
    )
    packed = jnp.where(token_valid[:, None] > 0, packed, jnp.zeros_like(packed))

    out_cols = lax.all_to_all(out_weight, "tp", 1, 0, tiled=True)
    prev_slot = passed_along(page_slot, "seq", 1)

    q_hm = jnp.transpose(queries, (1, 0, 2))
    kv_hm = jnp.transpose(packed.reshape(row_count, local_heads, 2 * HD), (1, 0, 2))
    seg_col = segment_start[:, None]
    valid_row = token_valid[None, :]
    seg_last = segment_start[row_count - 1]

    meta = jnp.stack([first_row, 1, seg_last]).astype(jnp.int32)
    split = local_heads // 2

    def absorb(state, incoming, step):
        step_arr = jnp.asarray(step, jnp.int32).reshape(1)
        return attend_step(step_arr, meta, valid_row, seg_col, q_hm, incoming[0], incoming[1], state)

    lane = jnp.arange(2 * HD, dtype=jnp.int32)
    initial = jnp.broadcast_to(
        jnp.where(lane == 0, -1e30, 0.0).astype(jnp.float32), (local_heads, row_count, 2 * HD)
    )

    own = (kv_hm[:split], kv_hm[split:])
    prev_block = tuple(lax.ppermute(part, "seq", chain) for part in own)
    carried = absorb(initial, own, 0)

    def step_with(pairs):
        def advance(step_index, carry_in):
            held, state = carry_in
            sent = tuple(lax.ppermute(part, "seq", pairs) for part in held)
            state = absorb(state, held, step_index)
            return (sent, state)

        return advance

    held, carried = lax.fori_loop(1, cross_steps, step_with(chain), (prev_block, carried))
    held, carried = lax.fori_loop(cross_steps, reach_dev, step_with(inner), (held, carried))
    carried = absorb(carried, held, reach_dev)
    attended = (
        jnp.transpose(carried[:, :, HD:] / carried[:, :, 1:2], (1, 0, 2))
        .astype(jnp.bfloat16)
        .reshape(row_count, local_heads * HD)
    )

    tiles = page_slot.shape[0]
    slot_count = 2 * tiles
    base_slot = seq_rank * slot_count
    has_prev = seq_rank > 0
    cand_slot = jnp.concatenate([page_slot, jnp.where(has_prev, prev_slot, -1)]) - base_slot
    cand_pages = jnp.concatenate(
        [packed.reshape(tiles, PAGE, -1), jnp.transpose(jnp.concatenate(prev_block, axis=0), (1, 0, 2)).reshape(tiles, PAGE, -1)],
        axis=0,
    )
    match = cand_slot[None, :] == jnp.arange(slot_count, dtype=jnp.int32)[:, None]
    pick = jnp.argmax(match.astype(jnp.int32), axis=1)
    found = jnp.any(match, axis=1)
    cache_pages = jnp.where(found[:, None, None], cand_pages[pick], jnp.zeros_like(cand_pages[:1]))

    attended_all = tp_gather(attended, tp_count)
    projected = jnp.dot(attended_all, out_cols, preferred_element_type=jnp.float32)
    hidden = (residual.astype(jnp.float32) + projected).astype(jnp.bfloat16)
    return (hidden, cache_pages)


def solution(mesh):
    return jax.shard_map(
        body,
        mesh=mesh,
        in_specs=(
            P("seq", "tp"),
            P(),
            P(None, "tp"),
            P(None, "tp"),
            P(None, "tp"),
            P("tp", None),
            P("seq"),
            P("seq"),
            P("seq"),
        ),
        out_specs=(P("seq", "tp"), P("seq", None, "tp")),
        check_vma=False,
    )
```

```python
import jax
import jax.numpy as jnp
from jax import lax
from jax.experimental import pallas as pl
from jax.experimental.pallas import tpu as pltpu
from jax.sharding import PartitionSpec as P

HD = 64
PAGE = 128
SPAN = 16


THETA = 130000.0
EPS = 1e-05
SCALE = HD ** (-0.5)
FAR = 1 << 30


def _step_kernel(step_ref, meta_ref, valid_ref, seg_ref, q_ref, kv_ref, s_ref, out_ref):
    rows, width = out_ref.shape
    keys = kv_ref.shape[0]
    step = step_ref[0]
    qstart = meta_ref[0]
    check_valid = jnp.where(step == 0, meta_ref[1], 0)
    seg_last = meta_ref[2]
    kstart = qstart - step * keys
    seg_first = seg_ref[0, 0]
    none_allowed = kstart + keys - 1 < seg_first
    all_allowed = (seg_last <= kstart) & (kstart + keys - 1 <= qstart) & (check_valid == 0)

    def update(allowed):
        q = q_ref[...]
        kv = kv_ref[...]
        scores = lax.dot_general(
            q, kv[:, :HD], (((1,), (1,)), ((), ())), preferred_element_type=jnp.float32
        ) * SCALE
        state = s_ref[...]
        m_old = state[:, 0:1]
        l_old = state[:, 1:2]
        if allowed is None:
            block_max = jnp.max(scores, axis=1, keepdims=True)
        else:
            block_max = jnp.max(jnp.where(allowed, scores, -1e30), axis=1, keepdims=True)
        m_new = jnp.maximum(m_old, block_max)
        weights = jnp.exp(scores - m_new)
        if allowed is not None:
            weights = jnp.where(allowed, weights, 0.0)
        shrink = jnp.exp(m_old - m_new)
        l_new = l_old * shrink + jnp.sum(weights, axis=1, keepdims=True)
        pv = jnp.dot(weights.astype(jnp.bfloat16), kv, preferred_element_type=jnp.float32)
        lane = lax.broadcasted_iota(jnp.int32, (rows, width), 1)
        acc = state * shrink + pv
        out_ref[...] = jnp.where(
            lane >= HD, acc, jnp.where(lane == 0, m_new, jnp.where(lane == 1, l_new, 0.0))
        )

    @pl.when(none_allowed)
    def _():
        out_ref[...] = s_ref[...]

    @pl.when(all_allowed & jnp.logical_not(none_allowed))
    def _():
        update(None)

    @pl.when(jnp.logical_not(all_allowed) & jnp.logical_not(none_allowed))
    def _():
        kpos = kstart + lax.broadcasted_iota(jnp.int32, (1, keys), 1)
        kpos = jnp.where((valid_ref[...] > 0) | (check_valid == 0), kpos, FAR)
        tpos = qstart + lax.broadcasted_iota(jnp.int32, (rows, 1), 0)
        update((kpos >= seg_ref[...]) & (kpos <= tpos))


def attend_step(step, meta, valid_row, seg_col, q_hm, kv_hm, state):
    heads, rows, _ = q_hm.shape
    keys = kv_hm.shape[1]
    width = kv_hm.shape[2]
    grid_spec = pltpu.PrefetchScalarGridSpec(
        num_scalar_prefetch=2,
        grid=(heads,),
        in_specs=[
            pl.BlockSpec((1, keys), lambda h, s, m: (0, 0)),
            pl.BlockSpec((rows, 1), lambda h, s, m: (0, 0)),
            pl.BlockSpec((None, rows, HD), lambda h, s, m: (h, 0, 0)),
            pl.BlockSpec((None, keys, width), lambda h, s, m: (h, 0, 0)),
            pl.BlockSpec((None, rows, width), lambda h, s, m: (h, 0, 0)),
        ],
        out_specs=pl.BlockSpec((None, rows, width), lambda h, s, m: (h, 0, 0)),
    )
    flops = heads * rows * keys * (2 * HD + 2 * width)
    return pl.pallas_call(
        _step_kernel,
        grid_spec=grid_spec,
        out_shape=jax.ShapeDtypeStruct(state.shape, jnp.float32),
        input_output_aliases={6: 0},
        cost_estimate=pl.CostEstimate(
            flops=flops,
            transcendentals=heads * rows * keys,
            bytes_accessed=q_hm.size * 2 + kv_hm.size * 2 + state.size * 8,
        ),
    )(step, meta, valid_row, seg_col, q_hm, kv_hm, state)


def tp_gather(x, count):
    copies = jnp.broadcast_to(x[None], (count,) + x.shape)
    got = lax.all_to_all(copies, "tp", 0, 0, tiled=True)
    return jnp.transpose(got, (1, 0, 2)).reshape(x.shape[0], count * x.shape[1])


def passed_along(x, axis, by):
    count = lax.axis_size(axis)
    pairs = [(i, i + by) for i in range(count) if 0 <= i + by < count]
    return lax.ppermute(x, axis, pairs)


def rotate(inputs, positions):
    half_dim = inputs.shape[-1] // 2
    frequency = THETA ** (-2.0 * jnp.arange(half_dim, dtype=jnp.float32) / inputs.shape[-1])
    angles = positions.astype(jnp.float32)[:, None] * frequency[None, :]
    cosine = jnp.cos(angles)[:, None, :]
    sine_part = jnp.sin(angles)[:, None, :]
    front_half = inputs[..., :half_dim]
    back_half = inputs[..., half_dim:]
    return jnp.concatenate(
        [front_half * cosine - back_half * sine_part, back_half * cosine + front_half * sine_part],
        axis=-1,
    )


def body(
    residual,
    norm_gain,
    query_weight,
    key_weight,
    value_weight,
    out_weight,
    segment_start,
    token_valid,
    page_slot,
):
    row_count = residual.shape[0]
    local_heads = query_weight.shape[1] // HD
    seq_rank = lax.axis_index("seq")
    seq_count = lax.axis_size("seq")
    reach_dev = min(SPAN, seq_count // 2)
    half = seq_count // 2
    chain = [(i, i + 1) for i in range(seq_count - 1)]
    inner = [p for p in chain if p != (half - 1, half)]
    first_block = segment_start[0] // row_count
    cross_here = jnp.clip(seq_rank - first_block, 0, reach_dev).astype(jnp.int32)
    told = jnp.broadcast_to(jnp.where(seq_rank == half, cross_here, 0), (seq_count,))
    cross_steps = jnp.sum(lax.all_to_all(told, "seq", 0, 0, tiled=True))
    cross_steps = jnp.maximum(cross_steps, 1)
    tp_count = lax.axis_size("tp")
    gathered = tp_gather(residual, tp_count)
    widened = gathered.astype(jnp.float32)
    mean_sq = jnp.mean(widened * widened, axis=1, keepdims=True)
    normed = (widened * lax.rsqrt(mean_sq + EPS) * norm_gain[None, :]).astype(jnp.bfloat16)
    seq_rank = lax.axis_index("seq")
    first_row = seq_rank * row_count
    places = first_row + jnp.arange(row_count, dtype=jnp.int32)
    offsets = places - segment_start
    queries = jnp.dot(normed, query_weight, preferred_element_type=jnp.float32).reshape(
        row_count, local_heads, HD
    )
    queries = rotate(queries, offsets).astype(jnp.bfloat16)
    key_rot = jnp.dot(normed, key_weight, preferred_element_type=jnp.float32).reshape(
        row_count, local_heads, HD
    )
    key_rot = rotate(key_rot, offsets).astype(jnp.bfloat16)
    values = (
        jnp.dot(normed, value_weight, preferred_element_type=jnp.float32)
        .reshape(row_count, local_heads, HD)
        .astype(jnp.bfloat16)
    )
    packed = jnp.concatenate([key_rot[:, :, None, :], values[:, :, None, :]], axis=2).reshape(
        row_count, local_heads * 2 * HD
    )
    packed = jnp.where(token_valid[:, None] > 0, packed, jnp.zeros_like(packed))

    out_cols = lax.all_to_all(out_weight, "tp", 1, 0, tiled=True)
    prev_slot = passed_along(page_slot, "seq", 1)

    q_hm = jnp.transpose(queries, (1, 0, 2))
    kv_hm = jnp.transpose(packed.reshape(row_count, local_heads, 2 * HD), (1, 0, 2))
    seg_col = segment_start[:, None]
    valid_row = token_valid[None, :]
    seg_last = segment_start[row_count - 1]

    meta = jnp.stack([first_row, 1, seg_last]).astype(jnp.int32)

    def absorb(state, incoming, step):
        step_arr = jnp.asarray(step, jnp.int32).reshape(1)
        return attend_step(step_arr, meta, valid_row, seg_col, q_hm, incoming, state)

    lane = jnp.arange(2 * HD, dtype=jnp.int32)
    initial = jnp.broadcast_to(
        jnp.where(lane == 0, -1e30, 0.0).astype(jnp.float32), (local_heads, row_count, 2 * HD)
    )

    prev_block = lax.ppermute(kv_hm, "seq", chain)
    carried = absorb(initial, kv_hm, 0)

    def step_with(pairs):
        def advance(step_index, carry_in):
            held, state = carry_in
            sent = lax.ppermute(held, "seq", pairs)
            state = absorb(state, held, step_index)
            return (sent, state)

        return advance

    held, carried = lax.fori_loop(1, cross_steps, step_with(chain), (prev_block, carried))
    held, carried = lax.fori_loop(cross_steps, reach_dev, step_with(inner), (held, carried))
    carried = absorb(carried, held, reach_dev)
    attended = (
        jnp.transpose(carried[:, :, HD:] / carried[:, :, 1:2], (1, 0, 2))
        .astype(jnp.bfloat16)
        .reshape(row_count, local_heads * HD)
    )

    tiles = page_slot.shape[0]
    slot_count = 2 * tiles
    base_slot = seq_rank * slot_count
    has_prev = seq_rank > 0
    cand_slot = jnp.concatenate([page_slot, jnp.where(has_prev, prev_slot, -1)]) - base_slot
    cand_pages = jnp.concatenate(
        [packed.reshape(tiles, PAGE, -1), jnp.transpose(prev_block, (1, 0, 2)).reshape(tiles, PAGE, -1)],
        axis=0,
    )
    match = cand_slot[None, :] == jnp.arange(slot_count, dtype=jnp.int32)[:, None]
    pick = jnp.argmax(match.astype(jnp.int32), axis=1)
    found = jnp.any(match, axis=1)
    cache_pages = jnp.where(found[:, None, None], cand_pages[pick], jnp.zeros_like(cand_pages[:1]))

    attended_all = tp_gather(attended, tp_count)
    projected = jnp.dot(attended_all, out_cols, preferred_element_type=jnp.float32)
    hidden = (residual.astype(jnp.float32) + projected).astype(jnp.bfloat16)
    return (hidden, cache_pages)


def solution(mesh):
    return jax.shard_map(
        body,
        mesh=mesh,
        in_specs=(
            P("seq", "tp"),
            P(),
            P(None, "tp"),
            P(None, "tp"),
            P(None, "tp"),
            P("tp", None),
            P("seq"),
            P("seq"),
            P("seq"),
        ),
        out_specs=(P("seq", "tp"), P("seq", None, "tp")),
        check_vma=False,
    )
```

```python
import jax
import jax.numpy as jnp
from jax import lax
from jax.experimental import pallas as pl
from jax.experimental.pallas import tpu as pltpu
from jax.sharding import PartitionSpec as P

HD = 64
PAGE = 128
SPAN = 16


THETA = 130000.0
EPS = 1e-05
SCALE = HD ** (-0.5)
FAR = 1 << 30


def _step_kernel(step_ref, meta_ref, valid_ref, seg_ref, q_ref, kv_ref, s_ref, out_ref):
    rows, width = out_ref.shape
    keys = kv_ref.shape[0]
    step = step_ref[0]
    qstart = meta_ref[0]
    check_valid = jnp.where(step == 0, meta_ref[1], 0)
    seg_last = meta_ref[2]
    kstart = qstart - step * keys
    seg_first = seg_ref[0, 0]
    none_allowed = kstart + keys - 1 < seg_first
    all_allowed = (seg_last <= kstart) & (kstart + keys - 1 <= qstart) & (check_valid == 0)

    def update(allowed):
        q = q_ref[...]
        kv = kv_ref[...]
        scores = lax.dot_general(
            q, kv[:, :HD], (((1,), (1,)), ((), ())), preferred_element_type=jnp.float32
        ) * SCALE
        state = s_ref[...]
        m_old = state[:, 0:1]
        l_old = state[:, 1:2]
        if allowed is None:
            block_max = jnp.max(scores, axis=1, keepdims=True)
        else:
            block_max = jnp.max(jnp.where(allowed, scores, -1e30), axis=1, keepdims=True)
        m_new = jnp.maximum(m_old, block_max)
        weights = jnp.exp(scores - m_new)
        if allowed is not None:
            weights = jnp.where(allowed, weights, 0.0)
        shrink = jnp.exp(m_old - m_new)
        l_new = l_old * shrink + jnp.sum(weights, axis=1, keepdims=True)
        pv = jnp.dot(weights.astype(jnp.bfloat16), kv, preferred_element_type=jnp.float32)
        lane = lax.broadcasted_iota(jnp.int32, (rows, width), 1)
        acc = state * shrink + pv
        out_ref[...] = jnp.where(
            lane >= HD, acc, jnp.where(lane == 0, m_new, jnp.where(lane == 1, l_new, 0.0))
        )

    @pl.when(none_allowed)
    def _():
        out_ref[...] = s_ref[...]

    @pl.when(all_allowed & jnp.logical_not(none_allowed))
    def _():
        update(None)

    @pl.when(jnp.logical_not(all_allowed) & jnp.logical_not(none_allowed))
    def _():
        kpos = kstart + lax.broadcasted_iota(jnp.int32, (1, keys), 1)
        kpos = jnp.where((valid_ref[...] > 0) | (check_valid == 0), kpos, FAR)
        tpos = qstart + lax.broadcasted_iota(jnp.int32, (rows, 1), 0)
        update((kpos >= seg_ref[...]) & (kpos <= tpos))


def attend_step(step, meta, valid_row, seg_col, q_hm, kv_hm, state):
    heads, rows, _ = q_hm.shape
    keys = kv_hm.shape[1]
    width = kv_hm.shape[2]
    grid_spec = pltpu.PrefetchScalarGridSpec(
        num_scalar_prefetch=2,
        grid=(heads,),
        in_specs=[
            pl.BlockSpec((1, keys), lambda h, s, m: (0, 0)),
            pl.BlockSpec((rows, 1), lambda h, s, m: (0, 0)),
            pl.BlockSpec((None, rows, HD), lambda h, s, m: (h, 0, 0)),
            pl.BlockSpec((None, keys, width), lambda h, s, m: (h, 0, 0)),
            pl.BlockSpec((None, rows, width), lambda h, s, m: (h, 0, 0)),
        ],
        out_specs=pl.BlockSpec((None, rows, width), lambda h, s, m: (h, 0, 0)),
    )
    flops = heads * rows * keys * (2 * HD + 2 * width)
    return pl.pallas_call(
        _step_kernel,
        grid_spec=grid_spec,
        out_shape=jax.ShapeDtypeStruct(state.shape, jnp.float32),
        input_output_aliases={6: 0},
        cost_estimate=pl.CostEstimate(
            flops=flops,
            transcendentals=heads * rows * keys,
            bytes_accessed=q_hm.size * 2 + kv_hm.size * 2 + state.size * 8,
        ),
    )(step, meta, valid_row, seg_col, q_hm, kv_hm, state)


def tp_gather(x, count):
    rank = lax.axis_index("tp")
    by_distance = [x] + [
        lax.ppermute(x, "tp", [(i, (i + s) % count) for i in range(count)]) for s in range(1, count)
    ]
    stacked = jnp.stack(by_distance)
    ordered = jnp.take(stacked, (rank - jnp.arange(count)) % count, axis=0)
    return jnp.transpose(ordered, (1, 0, 2)).reshape(x.shape[0], count * x.shape[1])


def passed_along(x, axis, by):
    count = lax.axis_size(axis)
    pairs = [(i, i + by) for i in range(count) if 0 <= i + by < count]
    return lax.ppermute(x, axis, pairs)


def rotate(inputs, positions):
    half_dim = inputs.shape[-1] // 2
    frequency = THETA ** (-2.0 * jnp.arange(half_dim, dtype=jnp.float32) / inputs.shape[-1])
    angles = positions.astype(jnp.float32)[:, None] * frequency[None, :]
    cosine = jnp.cos(angles)[:, None, :]
    sine_part = jnp.sin(angles)[:, None, :]
    front_half = inputs[..., :half_dim]
    back_half = inputs[..., half_dim:]
    return jnp.concatenate(
        [front_half * cosine - back_half * sine_part, back_half * cosine + front_half * sine_part],
        axis=-1,
    )


def body(
    residual,
    norm_gain,
    query_weight,
    key_weight,
    value_weight,
    out_weight,
    segment_start,
    token_valid,
    page_slot,
):
    row_count = residual.shape[0]
    local_heads = query_weight.shape[1] // HD
    seq_rank = lax.axis_index("seq")
    seq_count = lax.axis_size("seq")
    reach_dev = min(SPAN, seq_count // 2)
    half = seq_count // 2
    chain = [(i, i + 1) for i in range(seq_count - 1)]
    inner = [p for p in chain if p != (half - 1, half)]
    first_block = segment_start[0] // row_count
    cross_here = jnp.clip(seq_rank - first_block, 0, reach_dev).astype(jnp.int32)
    told = jnp.broadcast_to(jnp.where(seq_rank == half, cross_here, 0), (seq_count,))
    cross_steps = jnp.sum(lax.all_to_all(told, "seq", 0, 0, tiled=True))
    cross_steps = jnp.maximum(cross_steps, 1)
    tp_count = lax.axis_size("tp")
    gathered = tp_gather(residual, tp_count)
    widened = gathered.astype(jnp.float32)
    mean_sq = jnp.mean(widened * widened, axis=1, keepdims=True)
    normed = (widened * lax.rsqrt(mean_sq + EPS) * norm_gain[None, :]).astype(jnp.bfloat16)
    seq_rank = lax.axis_index("seq")
    first_row = seq_rank * row_count
    places = first_row + jnp.arange(row_count, dtype=jnp.int32)
    offsets = places - segment_start
    queries = jnp.dot(normed, query_weight, preferred_element_type=jnp.float32).reshape(
        row_count, local_heads, HD
    )
    queries = rotate(queries, offsets).astype(jnp.bfloat16)
    key_rot = jnp.dot(normed, key_weight, preferred_element_type=jnp.float32).reshape(
        row_count, local_heads, HD
    )
    key_rot = rotate(key_rot, offsets).astype(jnp.bfloat16)
    values = (
        jnp.dot(normed, value_weight, preferred_element_type=jnp.float32)
        .reshape(row_count, local_heads, HD)
        .astype(jnp.bfloat16)
    )
    packed = jnp.concatenate([key_rot[:, :, None, :], values[:, :, None, :]], axis=2).reshape(
        row_count, local_heads * 2 * HD
    )
    packed = jnp.where(token_valid[:, None] > 0, packed, jnp.zeros_like(packed))

    out_cols = lax.all_to_all(out_weight, "tp", 1, 0, tiled=True)
    prev_slot = passed_along(page_slot, "seq", 1)

    q_hm = jnp.transpose(queries, (1, 0, 2))
    kv_hm = jnp.transpose(packed.reshape(row_count, local_heads, 2 * HD), (1, 0, 2))
    seg_col = segment_start[:, None]
    valid_row = token_valid[None, :]
    seg_last = segment_start[row_count - 1]

    meta = jnp.stack([first_row, 1, seg_last]).astype(jnp.int32)

    def absorb(state, incoming, step):
        step_arr = jnp.asarray(step, jnp.int32).reshape(1)
        return attend_step(step_arr, meta, valid_row, seg_col, q_hm, incoming, state)

    lane = jnp.arange(2 * HD, dtype=jnp.int32)
    initial = jnp.broadcast_to(
        jnp.where(lane == 0, -1e30, 0.0).astype(jnp.float32), (local_heads, row_count, 2 * HD)
    )

    prev_block = lax.ppermute(kv_hm, "seq", chain)
    carried = absorb(initial, kv_hm, 0)

    def step_with(pairs):
        def advance(step_index, carry_in):
            held, state = carry_in
            sent = lax.ppermute(held, "seq", pairs)
            state = absorb(state, held, step_index)
            return (sent, state)

        return advance

    held, carried = lax.fori_loop(1, cross_steps, step_with(chain), (prev_block, carried))
    held, carried = lax.fori_loop(cross_steps, reach_dev, step_with(inner), (held, carried))
    carried = absorb(carried, held, reach_dev)
    attended = (
        jnp.transpose(carried[:, :, HD:] / carried[:, :, 1:2], (1, 0, 2))
        .astype(jnp.bfloat16)
        .reshape(row_count, local_heads * HD)
    )

    tiles = page_slot.shape[0]
    slot_count = 2 * tiles
    base_slot = seq_rank * slot_count
    has_prev = seq_rank > 0
    cand_slot = jnp.concatenate([page_slot, jnp.where(has_prev, prev_slot, -1)]) - base_slot
    cand_pages = jnp.concatenate(
        [packed.reshape(tiles, PAGE, -1), jnp.transpose(prev_block, (1, 0, 2)).reshape(tiles, PAGE, -1)],
        axis=0,
    )
    match = cand_slot[None, :] == jnp.arange(slot_count, dtype=jnp.int32)[:, None]
    pick = jnp.argmax(match.astype(jnp.int32), axis=1)
    found = jnp.any(match, axis=1)
    cache_pages = jnp.where(found[:, None, None], cand_pages[pick], jnp.zeros_like(cand_pages[:1]))

    attended_all = tp_gather(attended, tp_count)
    projected = jnp.dot(attended_all, out_cols, preferred_element_type=jnp.float32)
    hidden = (residual.astype(jnp.float32) + projected).astype(jnp.bfloat16)
    return (hidden, cache_pages)


def solution(mesh):
    return jax.shard_map(
        body,
        mesh=mesh,
        in_specs=(
            P("seq", "tp"),
            P(),
            P(None, "tp"),
            P(None, "tp"),
            P(None, "tp"),
            P("tp", None),
            P("seq"),
            P("seq"),
            P("seq"),
        ),
        out_specs=(P("seq", "tp"), P("seq", None, "tp")),
        check_vma=False,
    )
```

```python
import jax
import jax.numpy as jnp
from jax import lax
from jax.experimental import pallas as pl
from jax.experimental.pallas import tpu as pltpu
from jax.sharding import PartitionSpec as P

HD = 64
PAGE = 128
SPAN = 16


THETA = 130000.0
EPS = 1e-05
SCALE = HD ** (-0.5)
FAR = 1 << 30


def _step_kernel(step_ref, meta_ref, valid_ref, seg_ref, q_ref, kv_ref, s_ref, out_ref):
    rows, width = out_ref.shape
    keys = kv_ref.shape[0]
    step = step_ref[0]
    qstart = meta_ref[0]
    check_valid = jnp.where(step == 0, meta_ref[1], 0)
    seg_last = meta_ref[2]
    kstart = qstart - step * keys
    seg_first = seg_ref[0, 0]
    none_allowed = kstart + keys - 1 < seg_first
    all_allowed = (seg_last <= kstart) & (kstart + keys - 1 <= qstart) & (check_valid == 0)

    def update(allowed):
        q = q_ref[...]
        kv = kv_ref[...]
        scores = lax.dot_general(
            q, kv[:, :HD], (((1,), (1,)), ((), ())), preferred_element_type=jnp.float32
        ) * SCALE
        state = s_ref[...]
        m_old = state[:, 0:1]
        l_old = state[:, 1:2]
        if allowed is None:
            block_max = jnp.max(scores, axis=1, keepdims=True)
        else:
            block_max = jnp.max(jnp.where(allowed, scores, -1e30), axis=1, keepdims=True)
        m_new = jnp.maximum(m_old, block_max)
        weights = jnp.exp(scores - m_new)
        if allowed is not None:
            weights = jnp.where(allowed, weights, 0.0)
        shrink = jnp.exp(m_old - m_new)
        l_new = l_old * shrink + jnp.sum(weights, axis=1, keepdims=True)
        pv = jnp.dot(weights.astype(jnp.bfloat16), kv, preferred_element_type=jnp.float32)
        lane = lax.broadcasted_iota(jnp.int32, (rows, width), 1)
        acc = state * shrink + pv
        out_ref[...] = jnp.where(
            lane >= HD, acc, jnp.where(lane == 0, m_new, jnp.where(lane == 1, l_new, 0.0))
        )

    @pl.when(none_allowed)
    def _():
        out_ref[...] = s_ref[...]

    @pl.when(all_allowed & jnp.logical_not(none_allowed))
    def _():
        update(None)

    @pl.when(jnp.logical_not(all_allowed) & jnp.logical_not(none_allowed))
    def _():
        kpos = kstart + lax.broadcasted_iota(jnp.int32, (1, keys), 1)
        kpos = jnp.where((valid_ref[...] > 0) | (check_valid == 0), kpos, FAR)
        tpos = qstart + lax.broadcasted_iota(jnp.int32, (rows, 1), 0)
        update((kpos >= seg_ref[...]) & (kpos <= tpos))


def attend_step(step, meta, valid_row, seg_col, q_hm, kv_hm, state):
    heads, rows, _ = q_hm.shape
    keys = kv_hm.shape[1]
    width = kv_hm.shape[2]
    grid_spec = pltpu.PrefetchScalarGridSpec(
        num_scalar_prefetch=2,
        grid=(heads,),
        in_specs=[
            pl.BlockSpec((1, keys), lambda h, s, m: (0, 0)),
            pl.BlockSpec((rows, 1), lambda h, s, m: (0, 0)),
            pl.BlockSpec((None, rows, HD), lambda h, s, m: (h, 0, 0)),
            pl.BlockSpec((None, keys, width), lambda h, s, m: (h, 0, 0)),
            pl.BlockSpec((None, rows, width), lambda h, s, m: (h, 0, 0)),
        ],
        out_specs=pl.BlockSpec((None, rows, width), lambda h, s, m: (h, 0, 0)),
    )
    flops = heads * rows * keys * (2 * HD + 2 * width)
    return pl.pallas_call(
        _step_kernel,
        grid_spec=grid_spec,
        out_shape=jax.ShapeDtypeStruct(state.shape, jnp.float32),
        input_output_aliases={6: 0},
        cost_estimate=pl.CostEstimate(
            flops=flops,
            transcendentals=heads * rows * keys,
            bytes_accessed=q_hm.size * 2 + kv_hm.size * 2 + state.size * 8,
        ),
    )(step, meta, valid_row, seg_col, q_hm, kv_hm, state)


def tp_gather(x, count):
    rank = lax.axis_index("tp")
    by_distance = [x] + [
        lax.ppermute(x, "tp", [(i, (i + s) % count) for i in range(count)]) for s in range(1, count)
    ]
    stacked = jnp.stack(by_distance)
    ordered = jnp.take(stacked, (rank - jnp.arange(count)) % count, axis=0)
    return jnp.transpose(ordered, (1, 0, 2)).reshape(x.shape[0], count * x.shape[1])


def tp_columns(w, count):
    rank = lax.axis_index("tp")
    width = w.shape[1] // count
    pieces = [lax.dynamic_slice_in_dim(w, rank * width, width, axis=1)] + [
        lax.ppermute(
            lax.dynamic_slice_in_dim(w, ((rank + s) % count) * width, width, axis=1),
            "tp",
            [(i, (i + s) % count) for i in range(count)],
        )
        for s in range(1, count)
    ]
    stacked = jnp.stack(pieces)
    ordered = jnp.take(stacked, (rank - jnp.arange(count)) % count, axis=0)
    return ordered.reshape(count * w.shape[0], width)


def passed_along(x, axis, by):
    count = lax.axis_size(axis)
    pairs = [(i, i + by) for i in range(count) if 0 <= i + by < count]
    return lax.ppermute(x, axis, pairs)


def rotate(inputs, positions):
    half_dim = inputs.shape[-1] // 2
    frequency = THETA ** (-2.0 * jnp.arange(half_dim, dtype=jnp.float32) / inputs.shape[-1])
    angles = positions.astype(jnp.float32)[:, None] * frequency[None, :]
    cosine = jnp.cos(angles)[:, None, :]
    sine_part = jnp.sin(angles)[:, None, :]
    front_half = inputs[..., :half_dim]
    back_half = inputs[..., half_dim:]
    return jnp.concatenate(
        [front_half * cosine - back_half * sine_part, back_half * cosine + front_half * sine_part],
        axis=-1,
    )


def body(
    residual,
    norm_gain,
    query_weight,
    key_weight,
    value_weight,
    out_weight,
    segment_start,
    token_valid,
    page_slot,
):
    row_count = residual.shape[0]
    local_heads = query_weight.shape[1] // HD
    seq_rank = lax.axis_index("seq")
    seq_count = lax.axis_size("seq")
    reach_dev = min(SPAN, seq_count // 2)
    half = seq_count // 2
    chain = [(i, i + 1) for i in range(seq_count - 1)]
    inner = [p for p in chain if p != (half - 1, half)]
    first_block = segment_start[0] // row_count
    cross_here = jnp.clip(seq_rank - first_block, 0, reach_dev).astype(jnp.int32)
    told = jnp.broadcast_to(jnp.where(seq_rank == half, cross_here, 0), (seq_count,))
    cross_steps = jnp.sum(lax.all_to_all(told, "seq", 0, 0, tiled=True))
    cross_steps = jnp.maximum(cross_steps, 1)
    tp_count = lax.axis_size("tp")
    gathered = tp_gather(residual, tp_count)
    widened = gathered.astype(jnp.float32)
    mean_sq = jnp.mean(widened * widened, axis=1, keepdims=True)
    normed = (widened * lax.rsqrt(mean_sq + EPS) * norm_gain[None, :]).astype(jnp.bfloat16)
    seq_rank = lax.axis_index("seq")
    first_row = seq_rank * row_count
    places = first_row + jnp.arange(row_count, dtype=jnp.int32)
    offsets = places - segment_start
    queries = jnp.dot(normed, query_weight, preferred_element_type=jnp.float32).reshape(
        row_count, local_heads, HD
    )
    queries = rotate(queries, offsets).astype(jnp.bfloat16)
    key_rot = jnp.dot(normed, key_weight, preferred_element_type=jnp.float32).reshape(
        row_count, local_heads, HD
    )
    key_rot = rotate(key_rot, offsets).astype(jnp.bfloat16)
    values = (
        jnp.dot(normed, value_weight, preferred_element_type=jnp.float32)
        .reshape(row_count, local_heads, HD)
        .astype(jnp.bfloat16)
    )
    packed = jnp.concatenate([key_rot[:, :, None, :], values[:, :, None, :]], axis=2).reshape(
        row_count, local_heads * 2 * HD
    )
    packed = jnp.where(token_valid[:, None] > 0, packed, jnp.zeros_like(packed))

    out_cols = tp_columns(out_weight, lax.axis_size("tp"))
    prev_slot = passed_along(page_slot, "seq", 1)

    q_hm = jnp.transpose(queries, (1, 0, 2))
    kv_hm = jnp.transpose(packed.reshape(row_count, local_heads, 2 * HD), (1, 0, 2))
    seg_col = segment_start[:, None]
    valid_row = token_valid[None, :]
    seg_last = segment_start[row_count - 1]

    meta = jnp.stack([first_row, 1, seg_last]).astype(jnp.int32)

    def absorb(state, incoming, step):
        step_arr = jnp.asarray(step, jnp.int32).reshape(1)
        return attend_step(step_arr, meta, valid_row, seg_col, q_hm, incoming, state)

    lane = jnp.arange(2 * HD, dtype=jnp.int32)
    initial = jnp.broadcast_to(
        jnp.where(lane == 0, -1e30, 0.0).astype(jnp.float32), (local_heads, row_count, 2 * HD)
    )

    prev_block = lax.ppermute(kv_hm, "seq", chain)
    carried = absorb(initial, kv_hm, 0)

    def step_with(pairs):
        def advance(step_index, carry_in):
            held, state = carry_in
            sent = lax.ppermute(held, "seq", pairs)
            state = absorb(state, held, step_index)
            return (sent, state)

        return advance

    held, carried = lax.fori_loop(1, cross_steps, step_with(chain), (prev_block, carried))
    held, carried = lax.fori_loop(cross_steps, reach_dev, step_with(inner), (held, carried))
    carried = absorb(carried, held, reach_dev)
    attended = (
        jnp.transpose(carried[:, :, HD:] / carried[:, :, 1:2], (1, 0, 2))
        .astype(jnp.bfloat16)
        .reshape(row_count, local_heads * HD)
    )

    tiles = page_slot.shape[0]
    slot_count = 2 * tiles
    base_slot = seq_rank * slot_count
    has_prev = seq_rank > 0
    cand_slot = jnp.concatenate([page_slot, jnp.where(has_prev, prev_slot, -1)]) - base_slot
    cand_pages = jnp.concatenate(
        [packed.reshape(tiles, PAGE, -1), jnp.transpose(prev_block, (1, 0, 2)).reshape(tiles, PAGE, -1)],
        axis=0,
    )
    match = cand_slot[None, :] == jnp.arange(slot_count, dtype=jnp.int32)[:, None]
    pick = jnp.argmax(match.astype(jnp.int32), axis=1)
    found = jnp.any(match, axis=1)
    cache_pages = jnp.where(found[:, None, None], cand_pages[pick], jnp.zeros_like(cand_pages[:1]))

    attended_all = tp_gather(attended, tp_count)
    projected = jnp.dot(attended_all, out_cols, preferred_element_type=jnp.float32)
    hidden = (residual.astype(jnp.float32) + projected).astype(jnp.bfloat16)
    return (hidden, cache_pages)


def solution(mesh):
    return jax.shard_map(
        body,
        mesh=mesh,
        in_specs=(
            P("seq", "tp"),
            P(),
            P(None, "tp"),
            P(None, "tp"),
            P(None, "tp"),
            P("tp", None),
            P("seq"),
            P("seq"),
            P("seq"),
        ),
        out_specs=(P("seq", "tp"), P("seq", None, "tp")),
        check_vma=False,
    )
```

```python
import jax
import jax.numpy as jnp
from jax import lax
from jax.experimental import pallas as pl
from jax.experimental.pallas import tpu as pltpu
from jax.sharding import PartitionSpec as P

HD = 64
PAGE = 128
SPAN = 16


THETA = 130000.0
EPS = 1e-05
SCALE = HD ** (-0.5)
FAR = 1 << 30


def _step_kernel(step_ref, meta_ref, valid_ref, seg_ref, q_ref, kv_ref, s_ref, out_ref):
    rows, width = out_ref.shape
    keys = kv_ref.shape[0]
    step = step_ref[0]
    qstart = meta_ref[0]
    check_valid = jnp.where(step == 0, meta_ref[1], 0)
    seg_last = meta_ref[2]
    kstart = qstart - step * keys
    seg_first = seg_ref[0, 0]
    none_allowed = kstart + keys - 1 < seg_first
    all_allowed = (seg_last <= kstart) & (kstart + keys - 1 <= qstart) & (check_valid == 0)

    def update(allowed):
        q = q_ref[...]
        kv = kv_ref[...]
        scores = lax.dot_general(
            q, kv[:, :HD], (((1,), (1,)), ((), ())), preferred_element_type=jnp.float32
        ) * SCALE
        state = s_ref[...]
        m_old = state[:, 0:1]
        l_old = state[:, 1:2]
        if allowed is None:
            block_max = jnp.max(scores, axis=1, keepdims=True)
        else:
            block_max = jnp.max(jnp.where(allowed, scores, -1e30), axis=1, keepdims=True)
        m_new = jnp.maximum(m_old, block_max)
        weights = jnp.exp(scores - m_new)
        if allowed is not None:
            weights = jnp.where(allowed, weights, 0.0)
        shrink = jnp.exp(m_old - m_new)
        l_new = l_old * shrink + jnp.sum(weights, axis=1, keepdims=True)
        pv = jnp.dot(weights.astype(jnp.bfloat16), kv, preferred_element_type=jnp.float32)
        lane = lax.broadcasted_iota(jnp.int32, (rows, width), 1)
        acc = state * shrink + pv
        out_ref[...] = jnp.where(
            lane >= HD, acc, jnp.where(lane == 0, m_new, jnp.where(lane == 1, l_new, 0.0))
        )

    @pl.when(none_allowed)
    def _():
        out_ref[...] = s_ref[...]

    @pl.when(all_allowed & jnp.logical_not(none_allowed))
    def _():
        update(None)

    @pl.when(jnp.logical_not(all_allowed) & jnp.logical_not(none_allowed))
    def _():
        kpos = kstart + lax.broadcasted_iota(jnp.int32, (1, keys), 1)
        kpos = jnp.where((valid_ref[...] > 0) | (check_valid == 0), kpos, FAR)
        tpos = qstart + lax.broadcasted_iota(jnp.int32, (rows, 1), 0)
        update((kpos >= seg_ref[...]) & (kpos <= tpos))


def attend_step(step, meta, valid_row, seg_col, q_hm, kv_hm, state):
    heads, rows, _ = q_hm.shape
    keys = kv_hm.shape[1]
    width = kv_hm.shape[2]
    grid_spec = pltpu.PrefetchScalarGridSpec(
        num_scalar_prefetch=2,
        grid=(heads,),
        in_specs=[
            pl.BlockSpec((1, keys), lambda h, s, m: (0, 0)),
            pl.BlockSpec((rows, 1), lambda h, s, m: (0, 0)),
            pl.BlockSpec((None, rows, HD), lambda h, s, m: (h, 0, 0)),
            pl.BlockSpec((None, keys, width), lambda h, s, m: (h, 0, 0)),
            pl.BlockSpec((None, rows, width), lambda h, s, m: (h, 0, 0)),
        ],
        out_specs=pl.BlockSpec((None, rows, width), lambda h, s, m: (h, 0, 0)),
    )
    flops = heads * rows * keys * (2 * HD + 2 * width)
    return pl.pallas_call(
        _step_kernel,
        grid_spec=grid_spec,
        out_shape=jax.ShapeDtypeStruct(state.shape, jnp.float32),
        input_output_aliases={6: 0},
        cost_estimate=pl.CostEstimate(
            flops=flops,
            transcendentals=heads * rows * keys,
            bytes_accessed=q_hm.size * 2 + kv_hm.size * 2 + state.size * 8,
        ),
    )(step, meta, valid_row, seg_col, q_hm, kv_hm, state)


def tp_gather(x, count):
    rank = lax.axis_index("tp")
    by_distance = [x] + [
        lax.ppermute(x, "tp", [(i, (i + s) % count) for i in range(count)]) for s in range(1, count)
    ]
    stacked = jnp.stack(by_distance)
    ordered = jnp.take(stacked, (rank - jnp.arange(count)) % count, axis=0)
    return jnp.transpose(ordered, (1, 0, 2)).reshape(x.shape[0], count * x.shape[1])


def passed_along(x, axis, by):
    count = lax.axis_size(axis)
    pairs = [(i, i + by) for i in range(count) if 0 <= i + by < count]
    return lax.ppermute(x, axis, pairs)


def rotate(inputs, positions):
    half_dim = inputs.shape[-1] // 2
    frequency = THETA ** (-2.0 * jnp.arange(half_dim, dtype=jnp.float32) / inputs.shape[-1])
    angles = positions.astype(jnp.float32)[:, None] * frequency[None, :]
    cosine = jnp.cos(angles)[:, None, :]
    sine_part = jnp.sin(angles)[:, None, :]
    front_half = inputs[..., :half_dim]
    back_half = inputs[..., half_dim:]
    return jnp.concatenate(
        [front_half * cosine - back_half * sine_part, back_half * cosine + front_half * sine_part],
        axis=-1,
    )


def body(
    residual,
    norm_gain,
    query_weight,
    key_weight,
    value_weight,
    out_weight,
    segment_start,
    token_valid,
    page_slot,
):
    row_count = residual.shape[0]
    local_heads = query_weight.shape[1] // HD
    seq_rank = lax.axis_index("seq")
    seq_count = lax.axis_size("seq")
    reach_dev = min(SPAN, seq_count // 2)
    half = seq_count // 2
    chain = [(i, i + 1) for i in range(seq_count - 1)]
    inner = [p for p in chain if p != (half - 1, half)]
    first_block = segment_start[0] // row_count
    cross_here = jnp.clip(seq_rank - first_block, 0, reach_dev).astype(jnp.int32)
    told = jnp.broadcast_to(jnp.where(seq_rank == half, cross_here, 0), (seq_count,))
    cross_steps = jnp.sum(lax.all_to_all(told, "seq", 0, 0, tiled=True))
    cross_steps = jnp.maximum(cross_steps, 1)
    tp_count = lax.axis_size("tp")
    gathered = tp_gather(residual, tp_count)
    widened = gathered.astype(jnp.float32)
    mean_sq = jnp.mean(widened * widened, axis=1, keepdims=True)
    normed = (widened * lax.rsqrt(mean_sq + EPS) * norm_gain[None, :]).astype(jnp.bfloat16)
    seq_rank = lax.axis_index("seq")
    first_row = seq_rank * row_count
    places = first_row + jnp.arange(row_count, dtype=jnp.int32)
    offsets = places - segment_start
    queries = jnp.dot(normed, query_weight, preferred_element_type=jnp.float32).reshape(
        row_count, local_heads, HD
    )
    queries = rotate(queries, offsets).astype(jnp.bfloat16)
    key_rot = jnp.dot(normed, key_weight, preferred_element_type=jnp.float32).reshape(
        row_count, local_heads, HD
    )
    key_rot = rotate(key_rot, offsets).astype(jnp.bfloat16)
    values = (
        jnp.dot(normed, value_weight, preferred_element_type=jnp.float32)
        .reshape(row_count, local_heads, HD)
        .astype(jnp.bfloat16)
    )
    packed = jnp.concatenate([key_rot[:, :, None, :], values[:, :, None, :]], axis=2).reshape(
        row_count, local_heads * 2 * HD
    )
    packed = jnp.where(token_valid[:, None] > 0, packed, jnp.zeros_like(packed))

    prev_slot = passed_along(page_slot, "seq", 1)

    q_hm = jnp.transpose(queries, (1, 0, 2))
    kv_hm = jnp.transpose(packed.reshape(row_count, local_heads, 2 * HD), (1, 0, 2))
    seg_col = segment_start[:, None]
    valid_row = token_valid[None, :]
    seg_last = segment_start[row_count - 1]

    meta = jnp.stack([first_row, 1, seg_last]).astype(jnp.int32)

    def absorb(state, incoming, step):
        step_arr = jnp.asarray(step, jnp.int32).reshape(1)
        return attend_step(step_arr, meta, valid_row, seg_col, q_hm, incoming, state)

    lane = jnp.arange(2 * HD, dtype=jnp.int32)
    initial = jnp.broadcast_to(
        jnp.where(lane == 0, -1e30, 0.0).astype(jnp.float32), (local_heads, row_count, 2 * HD)
    )

    prev_block = lax.ppermute(kv_hm, "seq", chain)
    carried = absorb(initial, kv_hm, 0)

    def step_with(pairs):
        def advance(step_index, carry_in):
            held, state = carry_in
            sent = lax.ppermute(held, "seq", pairs)
            state = absorb(state, held, step_index)
            return (sent, state)

        return advance

    held, carried = lax.fori_loop(1, cross_steps, step_with(chain), (prev_block, carried))
    held, carried = lax.fori_loop(cross_steps, reach_dev, step_with(inner), (held, carried))
    carried = absorb(carried, held, reach_dev)
    attended = (
        jnp.transpose(carried[:, :, HD:] / carried[:, :, 1:2], (1, 0, 2))
        .astype(jnp.bfloat16)
        .reshape(row_count, local_heads * HD)
    )

    tiles = page_slot.shape[0]
    slot_count = 2 * tiles
    base_slot = seq_rank * slot_count
    has_prev = seq_rank > 0
    cand_slot = jnp.concatenate([page_slot, jnp.where(has_prev, prev_slot, -1)]) - base_slot
    cand_pages = jnp.concatenate(
        [packed.reshape(tiles, PAGE, -1), jnp.transpose(prev_block, (1, 0, 2)).reshape(tiles, PAGE, -1)],
        axis=0,
    )
    match = cand_slot[None, :] == jnp.arange(slot_count, dtype=jnp.int32)[:, None]
    pick = jnp.argmax(match.astype(jnp.int32), axis=1)
    found = jnp.any(match, axis=1)
    cache_pages = jnp.where(found[:, None, None], cand_pages[pick], jnp.zeros_like(cand_pages[:1]))

    out_late, attended = lax.optimization_barrier((out_weight, attended))
    out_cols = lax.all_to_all(out_late, "tp", 1, 0, tiled=True)
    attended_all = tp_gather(attended, tp_count)
    projected = jnp.dot(attended_all, out_cols, preferred_element_type=jnp.float32)
    hidden = (residual.astype(jnp.float32) + projected).astype(jnp.bfloat16)
    return (hidden, cache_pages)


def solution(mesh):
    return jax.shard_map(
        body,
        mesh=mesh,
        in_specs=(
            P("seq", "tp"),
            P(),
            P(None, "tp"),
            P(None, "tp"),
            P(None, "tp"),
            P("tp", None),
            P("seq"),
            P("seq"),
            P("seq"),
        ),
        out_specs=(P("seq", "tp"), P("seq", None, "tp")),
        check_vma=False,
    )
```
